256 devices in a mesh: sec: 16 (over x, y), mpo: 16 (over z, core).
Axes of the slice: x: 4, y: 4, z: 8, core: 2. Of those that a mesh axis runs over, the one named last changes fastest.
Arguments:
- theta: float32 [32, 8, 256, 256], P('sec'), may hold values from -6 to 6
- left_env: float32 [16, 32, 256, 256], P('mpo', 'sec'), may hold values from -0.5 to 0.5
- right_env: float32 [16, 32, 256, 256], P('mpo', 'sec'), may hold values from -0.375 to 0.375
- coeffs: float32 [16, 16], P('mpo'), may hold values from -1.5 to 1.5
- live_states: int32 [32, 8], replicated, may hold values from 0 to 15, all different within a row
- dest_device: int32 [32, 8, 1], replicated, may hold values from 0 to 15; in each aligned block of 16 rows (0 to 15, 16 to 31, ..., all dimensions but the last counted through in order) at most 2 rows name the same one
- dest_local: int32 [32, 8], replicated, may hold values from 0 to 1
Outputs:
- h_theta: float32 [32, 8, 256, 256], P('sec', None, 'mpo')
The draws below stay inside these ranges and needn't reach their ends.
Inputs may be any that keep to these rules, and one draw needn't show every extreme that they name: `dest_device`: within the rows of one device (aligned blocks of 16 entries, in order) no value appears more than 2 times, and some block has a value exactly 2 times. `live_states`: each row names 8 different states.
All inputs are finite; a program needn't handle non-finite values.
Results may differ from the reference program's by a relative error of at most 0.00007.
Values sent between devices are 32-bit elements; how exact they have to be, the bound alone decides.
No kernel may reach another device: no remote copies, remote signals or barrier semaphores. Data moves between devices by JAX's collectives and lax.ppermute only.
A program may use at most 128 MiB of HBM per device.

```python
import math
import jax
import jax.numpy as jnp
import numpy as np
from jax import lax

BD = 256
SEC_DEV = 2
STATES = 16
TOP = 8
NS = 32
K = 16
CAP = 2
N_SEC = 16


def plant(values, rng, smallest, top_value):
    index_at = [jax.random.randint(jax.random.fold_in(rng, axis), (), 0, length) for axis, length in enumerate(values.shape)]
    main_axis = values.shape.index(max(values.shape))
    next_to = index_at[:main_axis] + [(index_at[main_axis] + 1) % values.shape[main_axis]] + index_at[main_axis + 1:]
    return values.at[tuple(index_at)].set(smallest).at[tuple(next_to)].set(top_value)


def spiked(result, own_key, source, target, parts, factor):
    owner, partner = [(jnp.arange(result.shape[axis_at]) // (result.shape[axis_at] // parts)).reshape([-1 if axis == axis_at else 1 for axis in range(result.ndim)]) for axis_at in (source, target)]
    chosen = jax.random.permutation(own_key, parts)[partner]
    strong = (owner == chosen) | (owner == (partner + parts // 2) % parts)
    return jnp.where(strong, factor * result, result)


def shard_levels(stream_key, shape, shards, least, top_value):
    loudness, own = 1.0, jax.random.fold_in(stream_key, 6)
    for position, shards_of in shards:
        draws = jnp.exp(jax.random.uniform(jax.random.fold_in(own, position), (shards_of,), jnp.float32, least / len(shards), top_value / len(shards)))
        loudness = loudness * jnp.repeat(draws, shape[position] // shards_of).reshape([-1 if axis == position else 1 for axis in range(len(shape))])
    return loudness


def choose_distinct(rng, rows, number_of, top, lift):
    sequence = jax.random.permutation(jax.random.fold_in(rng, 1), number_of)
    favour = sequence
    for power in range(3):
        favour = favour * favour // number_of
    favour = favour * lift // number_of
    lots = jax.random.randint(jax.random.fold_in(rng, 2), (rows, number_of), 0, 4096) + favour
    fixed_rows = jax.random.permutation(jax.random.fold_in(rng, 3), rows)[jnp.arange(number_of) % rows]
    lots = jnp.where(jnp.arange(rows)[:, None] == fixed_rows[None, :], 1 << 14, lots)
    score = lots * number_of + jnp.arange(number_of)
    return lax.top_k(score.astype(jnp.int32), top)[1].astype(jnp.int32)


def assign_block(key, own, number, rows, count, top, most, skew):
    sequence = jax.random.permutation(key, count)
    heavy_load, ordinary = shares(count, rows * top, most, skew, True), shares(count, rows * top, most, skew, False)
    places = jnp.arange(count)

    def named(tallies, rotation):
        used = int((tallies > 0).sum())
        fixed = max(1, used // 4)
        moved = fixed + (places - fixed + rotation * (used - fixed)) % max(1, count - fixed)
        return jnp.zeros((count,), jnp.int32).at[sequence[jnp.where(places < fixed, places, moved)]].set(jnp.asarray(tallies, jnp.int32))

    tallies = jnp.where(number % 4 == 0, named(heavy_load, number // 4), named(ordinary, number - number // 4 - 1))
    mixed = jax.random.permutation(jax.random.fold_in(own, 3), count)
    source_of, receiver = mixed[0:count // 2 * 2:2], mixed[1:count // 2 * 2:2]
    margin = jnp.minimum(tallies[source_of] - 1, most - tallies[receiver]) // 2
    margin = jnp.where((source_of == sequence[0]) | (receiver == sequence[0]) | (tallies[receiver] == 0), 0, jnp.maximum(margin, 0))
    moved = jax.random.randint(jax.random.fold_in(own, 4), (count // 2,), 0, 1 << 20) % (margin + 1)
    tallies = tallies.at[source_of].add(-moved).at[receiver].add(moved)
    members = jnp.searchsorted(jnp.cumsum(tallies), jnp.arange(rows * top), side="right").astype(jnp.int32)
    grid = members.reshape(top, rows).T
    grid = grid[jax.random.permutation(jax.random.fold_in(own, 1), rows)]
    rotation = jax.random.randint(jax.random.fold_in(own, 2), (rows, 1), 0, top)
    return jnp.take_along_axis(grid, (jnp.arange(top)[None, :] + rotation) % top, axis=1)


def shares(number_of, total, most, skew, full):
    weights = [(1 << 20) // math.isqrt(standing ** skew) + 1 for standing in range(1, number_of + 1)]
    largest = most if full else min(most, max(-(-total // number_of), total * weights[0] // sum(weights)))
    least = 1 if total - largest >= number_of - 1 else 0
    holding, rest = [largest] + [least] * (number_of - 1), total - largest - least * (number_of - 1)
    while rest > 0:
        candidates = [i for i in range(1, number_of) if holding[i] < largest] or [i for i in range(1, number_of) if holding[i] < most]
        mass, left = sum([weights[i] for i in candidates]), rest
        for i in candidates:
            more = min(most - holding[i], max(1, left * weights[i] // mass), rest)
            holding[i] = holding[i] + more
            rest = rest - more
    return np.array(holding)


def scatter_about(key, extent, width, bound, pieces=(), dtype=jnp.bfloat16):
    drawn = width * jax.random.normal(key, extent, jnp.float32)
    if pieces:
        drawn = drawn * shard_levels(key, extent, pieces, -0.22, 0.18)
    return jnp.clip(drawn, -bound, bound).astype(dtype)


def noise_with(own_key, extent, deviation, reach, cuts, heavy, held_as=jnp.bfloat16):
    array = deviation * jax.random.normal(own_key, extent, jnp.float32)
    if cuts:
        array = array * shard_levels(own_key, extent, cuts, -0.22, 0.18)
    return jnp.clip(spiked(array, jax.random.fold_in(own_key, 3), *heavy), -reach, reach).astype(held_as)


def setup_inputs(seed: int = 0) -> dict:
    key_list = jax.random.split(jax.random.key(seed), 8)
    theta = scatter_about(key_list[0], (NS, TOP, BD, BD), 1.0, 6.0, ((0, 16),), jnp.float32)
    left_env = noise_with(key_list[1], (K, NS, BD, BD), BD ** -0.5, 0.5, ((0, 16), (1, 16)), (0, 3, 16, 2.0), jnp.float32)
    right_env = scatter_about(key_list[2], (K, NS, BD, BD), BD ** -0.5, 0.375, ((0, 16), (1, 16)), jnp.float32)
    coeffs = scatter_about(key_list[3], (K, STATES), 0.25, 1.5, ((0, 16),), jnp.float32)
    live_states = choose_distinct(key_list[4], NS, STATES, TOP, 0)
    dest_device_keys = jax.random.split(jax.random.fold_in(key_list[5], 1), NS * TOP // (SEC_DEV * TOP))
    dest_device_turns = jax.random.permutation(jax.random.fold_in(key_list[5], 3), NS * TOP // (SEC_DEV * TOP))
    dest_device = jax.vmap(lambda own, number: assign_block(jax.random.fold_in(key_list[5], 2), own, number, SEC_DEV * TOP, N_SEC, 1, CAP, 2))(dest_device_keys, dest_device_turns).reshape((NS, TOP, 1))
    dest_local = plant(jax.random.randint(key_list[6], (NS, TOP), 0, SEC_DEV), jax.random.fold_in(key_list[6], 1), 0, SEC_DEV - 1).astype(jnp.int32)
    return {"theta": theta, "left_env": left_env, "right_env": right_env, "coeffs": coeffs, "live_states": live_states, "dest_device": dest_device, "dest_local": dest_local}


def reference(theta, left_env, right_env, coeffs, live_states, dest_device, dest_local):
    right_sector = (dest_device[:, :, 0] * SEC_DEV + dest_local).astype(jnp.int32)
    weights = jnp.swapaxes(coeffs[:, live_states], 0, 1)
    lefts = jnp.swapaxes(left_env, 0, 1)

    def one_sector(items):
        block, left, right_ids, weight = items
        mixed = jnp.einsum('kac,jab->jkcb', left, block, precision=lax.Precision.HIGHEST)
        mixed = mixed * jnp.transpose(weight)[:, :, None, None]
        chosen = jnp.take(right_env, right_ids, axis=1)
        return jnp.einsum('jkcb,kjbd->jcd', mixed, chosen, precision=lax.Precision.HIGHEST)

    return lax.map(one_sector, (theta, lefts, right_sector, weights))
```

```python
import jax
import jax.numpy as jnp
from jax import lax
from jax.sharding import PartitionSpec as P


def shards(theta, left_env, right_env, coeffs, live_states, dest_device, dest_local):
    sec_dev, top, width = theta.shape[0], theta.shape[1], theta.shape[2]
    me_sec = lax.axis_index("sec")
    rights = lax.all_gather(right_env[0], "sec", axis=0, tiled=True)
    dev_mine = lax.dynamic_slice_in_dim(dest_device[:, :, 0], me_sec * sec_dev, sec_dev, 0)
    local_mine = lax.dynamic_slice_in_dim(dest_local, me_sec * sec_dev, sec_dev, 0)
    live_mine = lax.dynamic_slice_in_dim(live_states, me_sec * sec_dev, sec_dev, 0)
    right_sector = dev_mine * right_env.shape[1] + local_mine
    weight = jnp.take(coeffs[0], live_mine, axis=0)
    mixed = jnp.einsum("pac,pjab->pjcb", left_env[0], theta, precision=lax.Precision.HIGHEST)
    mixed = mixed * weight[:, :, None, None]
    chosen = jnp.take(rights, right_sector.reshape(-1), axis=0).reshape(sec_dev, top, width, width)
    part = jnp.einsum("pjcb,pjbd->pjcd", mixed, chosen, precision=lax.Precision.HIGHEST)
    return lax.psum_scatter(part, "mpo", scatter_dimension=2, tiled=True)


def solution(mesh):
    return jax.shard_map(
        shards,
        mesh=mesh,
        in_specs=(
            P("sec", None, None, None),
            P("mpo", "sec", None, None),
            P("mpo", "sec", None, None),
            P("mpo", None),
            P(),
            P(),
            P(),
        ),
        out_specs=P("sec", None, "mpo", None),
        check_vma=False,
    )
```

```python
import jax
import jax.numpy as jnp
from jax import lax
from jax.sharding import PartitionSpec as P

SIDE = 4


def torus_shift(axis, delta):
    pairs = []
    for x in range(SIDE):
        for y in range(SIDE):
            if axis == 0:
                pairs.append((x * SIDE + y, ((x + delta) % SIDE) * SIDE + y))
            else:
                pairs.append((x * SIDE + y, x * SIDE + (y + delta) % SIDE))
    return pairs


def ring_gather(block, axis):
    from_minus = lax.ppermute(block, "sec", torus_shift(axis, 1))
    from_plus = lax.ppermute(block, "sec", torus_shift(axis, -1))
    half = block.shape[-2] // 2
    far_low = lax.ppermute(from_minus[..., :half, :], "sec", torus_shift(axis, 1))
    far_high = lax.ppermute(from_plus[..., half:, :], "sec", torus_shift(axis, -1))
    far = jnp.concatenate([far_low, far_high], axis=-2)
    return jnp.stack([block, from_plus, far, from_minus])


def shards(theta, left_env, right_env, coeffs, live_states, dest_device, dest_local):
    sec_dev, top, width = theta.shape[0], theta.shape[1], theta.shape[2]
    me_sec = lax.axis_index("sec")
    mine = right_env[0]
    cut = width // 2
    first = ring_gather(ring_gather(mine[..., :cut], 0), 1).reshape(-1, width, cut)
    second = ring_gather(ring_gather(mine[..., cut:], 1), 0).reshape(-1, width, width - cut)
    dev_mine = lax.dynamic_slice_in_dim(dest_device[:, :, 0], me_sec * sec_dev, sec_dev, 0)
    local_mine = lax.dynamic_slice_in_dim(dest_local, me_sec * sec_dev, sec_dev, 0)
    live_mine = lax.dynamic_slice_in_dim(live_states, me_sec * sec_dev, sec_dev, 0)
    rel_x = (dev_mine // SIDE - me_sec // SIDE) % SIDE
    rel_y = (dev_mine % SIDE - me_sec % SIDE) % SIDE
    held = right_env.shape[1]
    index_first = ((rel_y * SIDE + rel_x) * held + local_mine).reshape(-1)
    index_second = ((rel_x * SIDE + rel_y) * held + local_mine).reshape(-1)
    weight = jnp.take(coeffs[0], live_mine, axis=0)
    mixed = jnp.einsum("pac,pjab->pjcb", left_env[0], theta, precision=lax.Precision.HIGHEST)
    mixed = mixed * weight[:, :, None, None]
    chosen = jnp.concatenate(
        [jnp.take(first, index_first, axis=0), jnp.take(second, index_second, axis=0)], axis=-1
    ).reshape(sec_dev, top, width, width)
    part = jnp.einsum("pjcb,pjbd->pjcd", mixed, chosen, precision=lax.Precision.HIGHEST)
    return lax.psum_scatter(part, "mpo", scatter_dimension=2, tiled=True)


def solution(mesh):
    return jax.shard_map(
        shards,
        mesh=mesh,
        in_specs=(
            P("sec", None, None, None),
            P("mpo", "sec", None, None),
            P("mpo", "sec", None, None),
            P("mpo", None),
            P(),
            P(),
            P(),
        ),
        out_specs=P("sec", None, "mpo", None),
        check_vma=False,
    )
```

```python
import jax
import jax.numpy as jnp
from jax import lax
from jax.sharding import PartitionSpec as P

SIDE = 4


def torus_shift(axis, delta):
    pairs = []
    for x in range(SIDE):
        for y in range(SIDE):
            if axis == 0:
                pairs.append((x * SIDE + y, ((x + delta) % SIDE) * SIDE + y))
            else:
                pairs.append((x * SIDE + y, x * SIDE + (y + delta) % SIDE))
    return pairs


def ring_gather(block, axis):
    from_minus = lax.ppermute(block, "sec", torus_shift(axis, 1))
    from_plus = lax.ppermute(block, "sec", torus_shift(axis, -1))
    half = block.shape[-2] // 2
    far_low = lax.ppermute(from_minus[..., :half, :], "sec", torus_shift(axis, 1))
    far_high = lax.ppermute(from_plus[..., half:, :], "sec", torus_shift(axis, -1))
    far = jnp.concatenate([far_low, far_high], axis=-2)
    return jnp.stack([block, from_plus, far, from_minus])


def shards(theta, left_env, right_env, coeffs, live_states, dest_device, dest_local):
    sec_dev, top, width = theta.shape[0], theta.shape[1], theta.shape[2]
    me_sec = lax.axis_index("sec")
    mine = right_env[0]
    held = right_env.shape[1]
    rows = width // 2
    dev_mine = lax.dynamic_slice_in_dim(dest_device[:, :, 0], me_sec * sec_dev, sec_dev, 0)
    local_mine = lax.dynamic_slice_in_dim(dest_local, me_sec * sec_dev, sec_dev, 0)
    live_mine = lax.dynamic_slice_in_dim(live_states, me_sec * sec_dev, sec_dev, 0)
    rel_x = (dev_mine // SIDE - me_sec // SIDE) % SIDE
    rel_y = (dev_mine % SIDE - me_sec % SIDE) % SIDE
    index_first = ((rel_y * SIDE + rel_x) * held + local_mine).reshape(-1)
    index_second = ((rel_x * SIDE + rel_y) * held + local_mine).reshape(-1)
    weight = jnp.take(coeffs[0], live_mine, axis=0)
    mixed = jnp.einsum("pac,pjab->pjcb", left_env[0], theta, precision=lax.Precision.HIGHEST)
    mixed = mixed * weight[:, :, None, None]
    chunks = 2
    cols = width // chunks
    pieces = []
    chosen = None
    for c in range(chunks):
        part_r = mine[:, :, c * cols:(c + 1) * cols]
        if chosen is not None:
            part_r, chosen = lax.optimization_barrier((part_r, chosen))
            pieces[-1] = pieces[-1](chosen)
        first = ring_gather(ring_gather(part_r[:, :rows], 0), 1).reshape(-1, rows, cols)
        second = ring_gather(ring_gather(part_r[:, rows:], 1), 0).reshape(-1, width - rows, cols)
        chosen = jnp.concatenate(
            [jnp.take(first, index_first, axis=0), jnp.take(second, index_second, axis=0)], axis=-2
        ).reshape(sec_dev, top, width, cols)
        pieces.append(lambda chosen: lax.psum_scatter(
            jnp.einsum("pjcb,pjbd->pjcd", mixed, chosen, precision=lax.Precision.HIGHEST),
            "mpo", scatter_dimension=2, tiled=True))
    pieces[-1] = pieces[-1](chosen)
    return jnp.concatenate(pieces, axis=-1)


def solution(mesh):
    return jax.shard_map(
        shards,
        mesh=mesh,
        in_specs=(
            P("sec", None, None, None),
            P("mpo", "sec", None, None),
            P("mpo", "sec", None, None),
            P("mpo", None),
            P(),
            P(),
            P(),
        ),
        out_specs=P("sec", None, "mpo", None),
        check_vma=False,
    )
```

```python
import jax
import jax.numpy as jnp
from jax import lax
from jax.sharding import PartitionSpec as P

SIDE = 4


def torus_shift(axis, delta):
    pairs = []
    for x in range(SIDE):
        for y in range(SIDE):
            if axis == 0:
                pairs.append((x * SIDE + y, ((x + delta) % SIDE) * SIDE + y))
            else:
                pairs.append((x * SIDE + y, x * SIDE + (y + delta) % SIDE))
    return pairs


def ring_gather(block, axis):
    from_minus = lax.ppermute(block, "sec", torus_shift(axis, 1))
    from_plus = lax.ppermute(block, "sec", torus_shift(axis, -1))
    half = block.shape[-2] // 2
    far_low = lax.ppermute(from_minus[..., :half, :], "sec", torus_shift(axis, 1))
    far_high = lax.ppermute(from_plus[..., half:, :], "sec", torus_shift(axis, -1))
    far = jnp.concatenate([far_low, far_high], axis=-2)
    return jnp.stack([block, from_plus, far, from_minus])


def shards(theta, left_env, right_env, coeffs, live_states, dest_device, dest_local):
    sec_dev, top, width = theta.shape[0], theta.shape[1], theta.shape[2]
    me_sec = lax.axis_index("sec")
    mine = right_env[0]
    cut = width // 2
    first = ring_gather(ring_gather(mine[..., :cut], 0), 1).reshape(-1, width, cut)
    second = ring_gather(ring_gather(mine[..., cut:], 1), 0).reshape(-1, width, width - cut)
    dev_mine = lax.dynamic_slice_in_dim(dest_device[:, :, 0], me_sec * sec_dev, sec_dev, 0)
    local_mine = lax.dynamic_slice_in_dim(dest_local, me_sec * sec_dev, sec_dev, 0)
    live_mine = lax.dynamic_slice_in_dim(live_states, me_sec * sec_dev, sec_dev, 0)
    rel_x = (dev_mine // SIDE - me_sec // SIDE) % SIDE
    rel_y = (dev_mine % SIDE - me_sec % SIDE) % SIDE
    held = right_env.shape[1]
    index_first = ((rel_y * SIDE + rel_x) * held + local_mine).reshape(-1)
    index_second = ((rel_x * SIDE + rel_y) * held + local_mine).reshape(-1)
    weight = jnp.take(coeffs[0], live_mine, axis=0)
    mixed = jnp.einsum("pac,pjab->pjcb", left_env[0], theta, precision=lax.Precision.HIGHEST)
    mixed = mixed * weight[:, :, None, None]
    chosen = jnp.concatenate(
        [jnp.take(first, index_first, axis=0), jnp.take(second, index_second, axis=0)], axis=-1
    ).reshape(sec_dev, top, width, width)
    part = jnp.einsum("pjcb,pjbd->pjcd", mixed, chosen, precision=lax.Precision.HIGHEST)
    return mpo_total(part)


def mpo_total(part):
    sec_dev, top, width = part.shape[0], part.shape[1], part.shape[2]
    planes = lax.axis_size("z")
    cores = lax.axis_size("core")
    rows = width // (planes * cores)
    grouped = part.reshape(sec_dev, top, planes, cores, rows, width)
    core = lax.axis_index("core")
    other = lax.dynamic_index_in_dim(grouped, 1 - core, 3, keepdims=False)
    keep = lax.dynamic_index_in_dim(grouped, core, 3, keepdims=False)
    arrived = lax.ppermute(other, "core", [(0, 1), (1, 0)])
    summed = keep + arrived
    total = lax.psum_scatter(summed, "z", scatter_dimension=2, tiled=True)
    return total.reshape(sec_dev, top, rows, width)


def solution(mesh):
    sec_size, mpo_size = mesh.devices.shape
    split = jax.sharding.Mesh(mesh.devices.reshape(sec_size, mpo_size // 2, 2), ("sec", "z", "core"))
    mpo = ("z", "core")
    return jax.shard_map(
        shards,
        mesh=split,
        in_specs=(
            P("sec", None, None, None),
            P(mpo, "sec", None, None),
            P(mpo, "sec", None, None),
            P(mpo, None),
            P(),
            P(),
            P(),
        ),
        out_specs=P("sec", None, mpo, None),
        check_vma=False,
    )
```

```python
import jax
import jax.numpy as jnp
from jax import lax
from jax.sharding import PartitionSpec as P

SIDE = 4


def torus_shift(axis, delta):
    pairs = []
    for x in range(SIDE):
        for y in range(SIDE):
            if axis == 0:
                pairs.append((x * SIDE + y, ((x + delta) % SIDE) * SIDE + y))
            else:
                pairs.append((x * SIDE + y, x * SIDE + (y + delta) % SIDE))
    return pairs


def ring_gather(block, axis):
    from_minus = lax.ppermute(block, "sec", torus_shift(axis, 1))
    from_plus = lax.ppermute(block, "sec", torus_shift(axis, -1))
    half = block.shape[-2] // 2
    far_low = lax.ppermute(from_minus[..., :half, :], "sec", torus_shift(axis, 1))
    far_high = lax.ppermute(from_plus[..., half:, :], "sec", torus_shift(axis, -1))
    far = jnp.concatenate([far_low, far_high], axis=-2)
    return jnp.stack([block, from_plus, far, from_minus])


def shards(theta, left_env, right_env, coeffs, live_states, dest_device, dest_local):
    sec_dev, top, width = theta.shape[0], theta.shape[1], theta.shape[2]
    me_sec = lax.axis_index("sec")
    mine = right_env[0]
    cut = width // 2
    first = lax.all_gather(mine[..., :cut], "sec", axis=0, tiled=True)
    second = ring_gather(ring_gather(mine[..., cut:], 1), 0).reshape(-1, width, width - cut)
    dev_mine = lax.dynamic_slice_in_dim(dest_device[:, :, 0], me_sec * sec_dev, sec_dev, 0)
    local_mine = lax.dynamic_slice_in_dim(dest_local, me_sec * sec_dev, sec_dev, 0)
    live_mine = lax.dynamic_slice_in_dim(live_states, me_sec * sec_dev, sec_dev, 0)
    rel_x = (dev_mine // SIDE - me_sec // SIDE) % SIDE
    rel_y = (dev_mine % SIDE - me_sec % SIDE) % SIDE
    held = right_env.shape[1]
    index_first = (dev_mine * held + local_mine).reshape(-1)
    index_second = ((rel_x * SIDE + rel_y) * held + local_mine).reshape(-1)
    weight = jnp.take(coeffs[0], live_mine, axis=0)
    mixed = jnp.einsum("pac,pjab->pjcb", left_env[0], theta, precision=lax.Precision.HIGHEST)
    mixed = mixed * weight[:, :, None, None]
    chosen = jnp.concatenate(
        [jnp.take(first, index_first, axis=0), jnp.take(second, index_second, axis=0)], axis=-1
    ).reshape(sec_dev, top, width, width)
    part = jnp.einsum("pjcb,pjbd->pjcd", mixed, chosen, precision=lax.Precision.HIGHEST)
    return mpo_total(part)


def mpo_total(part):
    sec_dev, top, width = part.shape[0], part.shape[1], part.shape[2]
    planes = lax.axis_size("z")
    cores = lax.axis_size("core")
    rows = width // (planes * cores)
    grouped = part.reshape(sec_dev, top, planes, cores, rows, width)
    core = lax.axis_index("core")
    other = lax.dynamic_index_in_dim(grouped, 1 - core, 3, keepdims=False)
    keep = lax.dynamic_index_in_dim(grouped, core, 3, keepdims=False)
    arrived = lax.ppermute(other, "core", [(0, 1), (1, 0)])
    summed = keep + arrived
    total = lax.psum_scatter(summed, "z", scatter_dimension=2, tiled=True)
    return total.reshape(sec_dev, top, rows, width)


def solution(mesh):
    sec_size, mpo_size = mesh.devices.shape
    split = jax.sharding.Mesh(mesh.devices.reshape(sec_size, mpo_size // 2, 2), ("sec", "z", "core"))
    mpo = ("z", "core")
    return jax.shard_map(
        shards,
        mesh=split,
        in_specs=(
            P("sec", None, None, None),
            P(mpo, "sec", None, None),
            P(mpo, "sec", None, None),
            P(mpo, None),
            P(),
            P(),
            P(),
        ),
        out_specs=P("sec", None, mpo, None),
        check_vma=False,
    )
```

```python
import jax
import jax.numpy as jnp
from jax import lax
from jax.sharding import PartitionSpec as P

SIDE = 4


def torus_shift(axis, delta):
    pairs = []
    for x in range(SIDE):
        for y in range(SIDE):
            if axis == 0:
                pairs.append((x * SIDE + y, ((x + delta) % SIDE) * SIDE + y))
            else:
                pairs.append((x * SIDE + y, x * SIDE + (y + delta) % SIDE))
    return pairs


def ring_gather(block, axis):
    from_minus = lax.ppermute(block, "sec", torus_shift(axis, 1))
    from_plus = lax.ppermute(block, "sec", torus_shift(axis, -1))
    half = block.shape[-2] // 2
    far_low = lax.ppermute(from_minus[..., :half, :], "sec", torus_shift(axis, 1))
    far_high = lax.ppermute(from_plus[..., half:, :], "sec", torus_shift(axis, -1))
    far = jnp.concatenate([far_low, far_high], axis=-2)
    return jnp.stack([block, from_plus, far, from_minus])


def shards(theta, left_env, right_env, coeffs, live_states, dest_device, dest_local):
    sec_dev, top, width = theta.shape[0], theta.shape[1], theta.shape[2]
    me_sec = lax.axis_index("sec")
    mine = right_env[0]
    cut = width // 2
    first = ring_gather(ring_gather(mine[..., :cut], 0), 1).reshape(-1, width, cut)
    second = ring_gather(ring_gather(mine[..., cut:], 1), 0).reshape(-1, width, width - cut)
    dev_mine = lax.dynamic_slice_in_dim(dest_device[:, :, 0], me_sec * sec_dev, sec_dev, 0)
    local_mine = lax.dynamic_slice_in_dim(dest_local, me_sec * sec_dev, sec_dev, 0)
    live_mine = lax.dynamic_slice_in_dim(live_states, me_sec * sec_dev, sec_dev, 0)
    rel_x = (dev_mine // SIDE - me_sec // SIDE) % SIDE
    rel_y = (dev_mine % SIDE - me_sec % SIDE) % SIDE
    held = right_env.shape[1]
    index_first = ((rel_y * SIDE + rel_x) * held + local_mine).reshape(-1)
    index_second = ((rel_x * SIDE + rel_y) * held + local_mine).reshape(-1)
    weight = jnp.take(coeffs[0], live_mine, axis=0)
    mixed = jnp.einsum("pac,pjab->pjcb", left_env[0], theta, precision=lax.Precision.HIGH)
    chosen = jnp.concatenate(
        [
            first.at[index_first].get(mode="promise_in_bounds"),
            second.at[index_second].get(mode="promise_in_bounds"),
        ],
        axis=-1,
    ).reshape(sec_dev, top, width, width)
    part = jnp.einsum("pjcb,pjbd->pjcd", mixed, chosen, precision=lax.Precision.HIGH)
    part = part * weight[:, :, None, None]
    return mpo_total(part)


def mpo_total(part):
    sec_dev, top, width = part.shape[0], part.shape[1], part.shape[2]
    planes = lax.axis_size("z")
    cores = lax.axis_size("core")
    rows = width // (planes * cores)
    grouped = part.reshape(sec_dev, top, planes, cores, rows, width)
    core = lax.axis_index("core")
    other = lax.dynamic_index_in_dim(grouped, 1 - core, 3, keepdims=False)
    keep = lax.dynamic_index_in_dim(grouped, core, 3, keepdims=False)
    arrived = lax.ppermute(other, "core", [(0, 1), (1, 0)])
    summed = keep + arrived
    total = lax.psum_scatter(summed, "z", scatter_dimension=2, tiled=True)
    return total.reshape(sec_dev, top, rows, width)


def solution(mesh):
    sec_size, mpo_size = mesh.devices.shape
    split = jax.sharding.Mesh(mesh.devices.reshape(sec_size, mpo_size // 2, 2), ("sec", "z", "core"))
    mpo = ("z", "core")
    return jax.shard_map(
        shards,
        mesh=split,
        in_specs=(
            P("sec", None, None, None),
            P(mpo, "sec", None, None),
            P(mpo, "sec", None, None),
            P(mpo, None),
            P(),
            P(),
            P(),
        ),
        out_specs=P("sec", None, mpo, None),
        check_vma=False,
    )
```

```python
import jax
import jax.numpy as jnp
from jax import lax
from jax.sharding import PartitionSpec as P
from jax.experimental import pallas as pl
from jax.experimental.pallas import tpu as pltpu

SIDE = 4


def torus_shift(axis, delta):
    pairs = []
    for x in range(SIDE):
        for y in range(SIDE):
            if axis == 0:
                pairs.append((x * SIDE + y, ((x + delta) % SIDE) * SIDE + y))
            else:
                pairs.append((x * SIDE + y, x * SIDE + (y + delta) % SIDE))
    return pairs


def ring_gather(block, axis):
    from_minus = lax.ppermute(block, "sec", torus_shift(axis, 1))
    from_plus = lax.ppermute(block, "sec", torus_shift(axis, -1))
    half = block.shape[-2] // 2
    far_low = lax.ppermute(from_minus[..., :half, :], "sec", torus_shift(axis, 1))
    far_high = lax.ppermute(from_plus[..., half:, :], "sec", torus_shift(axis, -1))
    return block, from_plus, far_low, far_high, from_minus


def ring_stack(block, axis):
    own, plus, far_low, far_high, minus = ring_gather(block, axis)
    return jnp.stack([own, plus, jnp.concatenate([far_low, far_high], axis=-2), minus])


def pick_kernel(sel_a, sub_a, sel_b, sub_b, weight, mixed, a0, a1, a2, a3, a4, b0, b1, b2, b3, b4, out, held, sems):
    step = pl.program_id(0)
    steps = pl.num_programs(0)
    rows, cols = a0.shape[1], a0.shape[2]
    half = a2.shape[1]
    sides = ((sel_a, sub_a, (a0, a1, a2, a3, a4)), (sel_b, sub_b, (b0, b1, b2, b3, b4)))

    def fetch(index, slot, wait):
        for side, (sel, sub, pieces) in enumerate(sides):
            own, plus, low, high, minus = pieces
            case, k = sel[index], sub[index]
            whole = held.at[slot, :, pl.ds(side * cols, cols)]
            top = held.at[slot, pl.ds(0, half), pl.ds(side * cols, cols)]
            bottom = held.at[slot, pl.ds(half, rows - half), pl.ds(side * cols, cols)]
            for number, src in ((0, own), (1, plus), (3, minus)):
                @pl.when(case == number)
                def _():
                    copy = pltpu.make_async_copy(src.at[k], whole, sems.at[slot, side, 0])
                    copy.wait() if wait else copy.start()

            @pl.when(case == 2)
            def _():
                first = pltpu.make_async_copy(low.at[k], top, sems.at[slot, side, 0])
                second = pltpu.make_async_copy(high.at[k], bottom, sems.at[slot, side, 1])
                if wait:
                    first.wait()
                    second.wait()
                else:
                    first.start()
                    second.start()

    slot = step % 2

    @pl.when(step == 0)
    def _():
        fetch(0, 0, False)

    @pl.when(step + 1 < steps)
    def _():
        fetch(step + 1, 1 - slot, False)

    fetch(step, slot, True)
    product = jnp.dot(mixed[0], held[slot], precision=lax.Precision.HIGHEST, preferred_element_type=jnp.float32)
    out[0] = product * weight[step]


def pick_product(mixed, weight, sel_a, sub_a, pieces_a, sel_b, sub_b, pieces_b):
    blocks, width = mixed.shape[0], mixed.shape[1]
    any_spec = pl.BlockSpec(memory_space=pl.ANY)
    grid_spec = pltpu.PrefetchScalarGridSpec(
        num_scalar_prefetch=5,
        grid=(blocks,),
        in_specs=[pl.BlockSpec((1, width, width), lambda i, *_: (i, 0, 0))] + [any_spec] * 10,
        out_specs=pl.BlockSpec((1, width, width), lambda i, *_: (i, 0, 0)),
        scratch_shapes=[pltpu.VMEM((2, width, width), jnp.float32), pltpu.SemaphoreType.DMA((2, 2, 2))],
    )
    return pl.pallas_call(
        pick_kernel,
        grid_spec=grid_spec,
        out_shape=jax.ShapeDtypeStruct(mixed.shape, jnp.float32),
        compiler_params=pltpu.CompilerParams(dimension_semantics=("arbitrary",)),
        cost_estimate=pl.CostEstimate(
            flops=2 * blocks * width ** 3, transcendentals=0, bytes_accessed=3 * 4 * blocks * width * width
        ),
    )(sel_a, sub_a, sel_b, sub_b, weight, mixed, *pieces_a, *pieces_b)


def shards(theta, left_env, right_env, coeffs, live_states, dest_device, dest_local):
    sec_dev, top, width = theta.shape[0], theta.shape[1], theta.shape[2]
    me_sec = lax.axis_index("sec")
    mine = right_env[0]
    cut = width // 2
    held = right_env.shape[1]
    flat = lambda piece: piece.reshape(-1, piece.shape[-2], piece.shape[-1])
    pieces_a = [flat(p) for p in ring_gather(ring_stack(mine[..., :cut], 0), 1)]
    pieces_b = [flat(p) for p in ring_gather(ring_stack(mine[..., cut:], 1), 0)]
    dev_mine = lax.dynamic_slice_in_dim(dest_device[:, :, 0], me_sec * sec_dev, sec_dev, 0)
    local_mine = lax.dynamic_slice_in_dim(dest_local, me_sec * sec_dev, sec_dev, 0)
    live_mine = lax.dynamic_slice_in_dim(live_states, me_sec * sec_dev, sec_dev, 0)
    rel_x = ((dev_mine // SIDE - me_sec // SIDE) % SIDE).reshape(-1)
    rel_y = ((dev_mine % SIDE - me_sec % SIDE) % SIDE).reshape(-1)
    local_flat = local_mine.reshape(-1)
    weight = jnp.take(coeffs[0], live_mine, axis=0).reshape(-1)
    mixed = jnp.einsum("pac,pjab->pjcb", left_env[0], theta, precision=lax.Precision.HIGH)
    part = pick_product(
        mixed.reshape(sec_dev * top, width, width), weight,
        rel_y, rel_x * held + local_flat, pieces_a,
        rel_x, rel_y * held + local_flat, pieces_b,
    ).reshape(sec_dev, top, width, width)
    return mpo_total(part)


def mpo_total(part):
    sec_dev, top, width = part.shape[0], part.shape[1], part.shape[2]
    planes = lax.axis_size("z")
    cores = lax.axis_size("core")
    rows = width // (planes * cores)
    grouped = part.reshape(sec_dev, top, planes, cores, rows, width)
    core = lax.axis_index("core")
    other = lax.dynamic_index_in_dim(grouped, 1 - core, 3, keepdims=False)
    keep = lax.dynamic_index_in_dim(grouped, core, 3, keepdims=False)
    arrived = lax.ppermute(other, "core", [(0, 1), (1, 0)])
    summed = keep + arrived
    total = lax.psum_scatter(summed, "z", scatter_dimension=2, tiled=True)
    return total.reshape(sec_dev, top, rows, width)


def solution(mesh):
    sec_size, mpo_size = mesh.devices.shape
    split = jax.sharding.Mesh(mesh.devices.reshape(sec_size, mpo_size // 2, 2), ("sec", "z", "core"))
    mpo = ("z", "core")
    return jax.shard_map(
        shards,
        mesh=split,
        in_specs=(
            P("sec", None, None, None),
            P(mpo, "sec", None, None),
            P(mpo, "sec", None, None),
            P(mpo, None),
            P(),
            P(),
            P(),
        ),
        out_specs=P("sec", None, mpo, None),
        check_vma=False,
    )
```

```python
import jax
import jax.numpy as jnp
from jax import lax
from jax.sharding import PartitionSpec as P
from jax.experimental import pallas as pl
from jax.experimental.pallas import tpu as pltpu

SIDE = 4


def torus_shift(axis, delta):
    pairs = []
    for x in range(SIDE):
        for y in range(SIDE):
            if axis == 0:
                pairs.append((x * SIDE + y, ((x + delta) % SIDE) * SIDE + y))
            else:
                pairs.append((x * SIDE + y, x * SIDE + (y + delta) % SIDE))
    return pairs


def ring_gather(block, axis):
    from_minus = lax.ppermute(block, "sec", torus_shift(axis, 1))
    from_plus = lax.ppermute(block, "sec", torus_shift(axis, -1))
    half = block.shape[-2] // 2
    far_low = lax.ppermute(from_minus[..., :half, :], "sec", torus_shift(axis, 1))
    far_high = lax.ppermute(from_plus[..., half:, :], "sec", torus_shift(axis, -1))
    return block, from_plus, far_low, far_high, from_minus


def ring_stack(block, axis):
    own, plus, far_low, far_high, minus = ring_gather(block, axis)
    return jnp.stack([own, plus, jnp.concatenate([far_low, far_high], axis=-2), minus])


def split_dot(a, b):
    a_high = a.astype(jnp.bfloat16)
    a_low = (a - a_high.astype(jnp.float32)).astype(jnp.bfloat16)
    b_high = b.astype(jnp.bfloat16)
    b_low = (b - b_high.astype(jnp.float32)).astype(jnp.bfloat16)
    dot = lambda x, y: jnp.dot(x, y, preferred_element_type=jnp.float32)
    return (dot(a_low, b_high) + dot(a_high, b_low)) + dot(a_high, b_high)


def pick_kernel(sel_a, sub_a, sel_b, sub_b, weight, lefts, theta, a0, a1, a2, a3, a4, b0, b1, b2, b3, b4, out, held, sems):
    step = pl.program_id(0)
    steps = pl.num_programs(0)
    rows, cols = a0.shape[1], a0.shape[2]
    half = a2.shape[1]
    sides = ((sel_a, sub_a, (a0, a1, a2, a3, a4)), (sel_b, sub_b, (b0, b1, b2, b3, b4)))

    def fetch(index, slot, wait):
        for side, (sel, sub, pieces) in enumerate(sides):
            own, plus, low, high, minus = pieces
            case, k = sel[index], sub[index]
            whole = held.at[slot, :, pl.ds(side * cols, cols)]
            top = held.at[slot, pl.ds(0, half), pl.ds(side * cols, cols)]
            bottom = held.at[slot, pl.ds(half, rows - half), pl.ds(side * cols, cols)]
            for number, src in ((0, own), (1, plus), (3, minus)):
                @pl.when(case == number)
                def _():
                    copy = pltpu.make_async_copy(src.at[k], whole, sems.at[slot, side, 0])
                    copy.wait() if wait else copy.start()

            @pl.when(case == 2)
            def _():
                first = pltpu.make_async_copy(low.at[k], top, sems.at[slot, side, 0])
                second = pltpu.make_async_copy(high.at[k], bottom, sems.at[slot, side, 1])
                if wait:
                    first.wait()
                    second.wait()
                else:
                    first.start()
                    second.start()

    slot = step % 2

    @pl.when(step == 0)
    def _():
        fetch(0, 0, False)

    @pl.when(step + 1 < steps)
    def _():
        fetch(step + 1, 1 - slot, False)

    mixed = split_dot(lefts[0], theta[0, 0])
    fetch(step, slot, True)
    out[0, 0] = split_dot(mixed, held[slot]) * weight[step]


def pick_product(lefts_t, theta, weight, sel_a, sub_a, pieces_a, sel_b, sub_b, pieces_b):
    sec_dev, top, width = theta.shape[0], theta.shape[1], theta.shape[2]
    blocks = sec_dev * top
    any_spec = pl.BlockSpec(memory_space=pl.ANY)
    grid_spec = pltpu.PrefetchScalarGridSpec(
        num_scalar_prefetch=5,
        grid=(blocks,),
        in_specs=[
            pl.BlockSpec((1, width, width), lambda i, *_: (i // top, 0, 0)),
            pl.BlockSpec((1, 1, width, width), lambda i, *_: (i // top, i % top, 0, 0)),
        ] + [any_spec] * 10,
        out_specs=pl.BlockSpec((1, 1, width, width), lambda i, *_: (i // top, i % top, 0, 0)),
        scratch_shapes=[pltpu.VMEM((2, width, width), jnp.float32), pltpu.SemaphoreType.DMA((2, 2, 2))],
    )
    return pl.pallas_call(
        pick_kernel,
        grid_spec=grid_spec,
        out_shape=jax.ShapeDtypeStruct(theta.shape, jnp.float32),
        compiler_params=pltpu.CompilerParams(dimension_semantics=("arbitrary",)),
        cost_estimate=pl.CostEstimate(
            flops=12 * blocks * width ** 3, transcendentals=0, bytes_accessed=3 * 4 * blocks * width * width
        ),
    )(sel_a, sub_a, sel_b, sub_b, weight, lefts_t, theta, *pieces_a, *pieces_b)


def shards(theta, left_env, right_env, coeffs, live_states, dest_device, dest_local):
    sec_dev, top, width = theta.shape[0], theta.shape[1], theta.shape[2]
    me_sec = lax.axis_index("sec")
    mine = right_env[0]
    cut = width // 2
    held = right_env.shape[1]
    flat = lambda piece: piece.reshape(-1, piece.shape[-2], piece.shape[-1])
    pieces_a = [flat(p) for p in ring_gather(ring_stack(mine[..., :cut], 0), 1)]
    pieces_b = [flat(p) for p in ring_gather(ring_stack(mine[..., cut:], 1), 0)]
    dev_mine = lax.dynamic_slice_in_dim(dest_device[:, :, 0], me_sec * sec_dev, sec_dev, 0)
    local_mine = lax.dynamic_slice_in_dim(dest_local, me_sec * sec_dev, sec_dev, 0)
    live_mine = lax.dynamic_slice_in_dim(live_states, me_sec * sec_dev, sec_dev, 0)
    rel_x = ((dev_mine // SIDE - me_sec // SIDE) % SIDE).reshape(-1)
    rel_y = ((dev_mine % SIDE - me_sec % SIDE) % SIDE).reshape(-1)
    local_flat = local_mine.reshape(-1)
    weight = jnp.take(coeffs[0], live_mine, axis=0).reshape(-1)
    lefts_t = jnp.swapaxes(left_env[0], 1, 2)
    part = pick_product(
        lefts_t, theta, weight,
        rel_y, rel_x * held + local_flat, pieces_a,
        rel_x, rel_y * held + local_flat, pieces_b,
    )
    return mpo_total(part)


def mpo_total(part):
    sec_dev, top, width = part.shape[0], part.shape[1], part.shape[2]
    planes = lax.axis_size("z")
    cores = lax.axis_size("core")
    rows = width // (planes * cores)
    grouped = part.reshape(sec_dev, top, planes, cores, rows, width)
    core = lax.axis_index("core")
    other = lax.dynamic_index_in_dim(grouped, 1 - core, 3, keepdims=False)
    keep = lax.dynamic_index_in_dim(grouped, core, 3, keepdims=False)
    arrived = lax.ppermute(other, "core", [(0, 1), (1, 0)])
    summed = keep + arrived
    total = lax.psum_scatter(summed, "z", scatter_dimension=2, tiled=True)
    return total.reshape(sec_dev, top, rows, width)


def solution(mesh):
    sec_size, mpo_size = mesh.devices.shape
    split = jax.sharding.Mesh(mesh.devices.reshape(sec_size, mpo_size // 2, 2), ("sec", "z", "core"))
    mpo = ("z", "core")
    return jax.shard_map(
        shards,
        mesh=split,
        in_specs=(
            P("sec", None, None, None),
            P(mpo, "sec", None, None),
            P(mpo, "sec", None, None),
            P(mpo, None),
            P(),
            P(),
            P(),
        ),
        out_specs=P("sec", None, mpo, None),
        check_vma=False,
    )
```

```python
import jax
import jax.numpy as jnp
from jax import lax
from jax.sharding import PartitionSpec as P
from jax.experimental import pallas as pl
from jax.experimental.pallas import tpu as pltpu

SIDE = 4


def torus_shift(axis, delta):
    pairs = []
    for x in range(SIDE):
        for y in range(SIDE):
            if axis == 0:
                pairs.append((x * SIDE + y, ((x + delta) % SIDE) * SIDE + y))
            else:
                pairs.append((x * SIDE + y, x * SIDE + (y + delta) % SIDE))
    return pairs


def ring_gather(block, axis):
    from_minus = lax.ppermute(block, "sec", torus_shift(axis, 1))
    from_plus = lax.ppermute(block, "sec", torus_shift(axis, -1))
    half = block.shape[-2] // 2
    far_low = lax.ppermute(from_minus[..., :half, :], "sec", torus_shift(axis, 1))
    far_high = lax.ppermute(from_plus[..., half:, :], "sec", torus_shift(axis, -1))
    return block, from_plus, far_low, far_high, from_minus


def ring_stack(block, axis):
    own, plus, far_low, far_high, minus = ring_gather(block, axis)
    return jnp.stack([own, plus, jnp.concatenate([far_low, far_high], axis=-2), minus])


def split_dot(a, b):
    a_high = a.astype(jnp.bfloat16)
    a_low = (a - a_high.astype(jnp.float32)).astype(jnp.bfloat16)
    b_high = b.astype(jnp.bfloat16)
    b_low = (b - b_high.astype(jnp.float32)).astype(jnp.bfloat16)
    dot = lambda x, y: jnp.dot(x, y, preferred_element_type=jnp.float32)
    return (dot(a_low, b_high) + dot(a_high, b_low)) + dot(a_high, b_high)


def pick_kernel(sel_a, sub_a, sel_b, sub_b, weight, mixed, a0, a1, a2, a3, a4, b0, b1, b2, b3, b4, out, held, sems):
    step = pl.program_id(0)
    steps = pl.num_programs(0)
    rows, cols = a0.shape[1], a0.shape[2]
    half = a2.shape[1]
    sides = ((sel_a, sub_a, (a0, a1, a2, a3, a4)), (sel_b, sub_b, (b0, b1, b2, b3, b4)))

    def fetch(index, slot, wait):
        for side, (sel, sub, pieces) in enumerate(sides):
            own, plus, low, high, minus = pieces
            case, k = sel[index], sub[index]
            whole = held.at[slot, :, pl.ds(side * cols, cols)]
            top = held.at[slot, pl.ds(0, half), pl.ds(side * cols, cols)]
            bottom = held.at[slot, pl.ds(half, rows - half), pl.ds(side * cols, cols)]
            for number, src in ((0, own), (1, plus), (3, minus)):
                @pl.when(case == number)
                def _():
                    copy = pltpu.make_async_copy(src.at[k], whole, sems.at[slot, side, 0])
                    copy.wait() if wait else copy.start()

            @pl.when(case == 2)
            def _():
                first = pltpu.make_async_copy(low.at[k], top, sems.at[slot, side, 0])
                second = pltpu.make_async_copy(high.at[k], bottom, sems.at[slot, side, 1])
                if wait:
                    first.wait()
                    second.wait()
                else:
                    first.start()
                    second.start()

    slot = step % 2

    @pl.when(step == 0)
    def _():
        fetch(0, 0, False)

    @pl.when(step + 1 < steps)
    def _():
        fetch(step + 1, 1 - slot, False)

    fetch(step, slot, True)
    out[0, 0] = split_dot(mixed[0, 0], held[slot]) * weight[step]


def pick_product(theta, weight, sel_a, sub_a, pieces_a, sel_b, sub_b, pieces_b):
    sec_dev, top, width = theta.shape[0], theta.shape[1], theta.shape[2]
    blocks = sec_dev * top
    any_spec = pl.BlockSpec(memory_space=pl.ANY)
    grid_spec = pltpu.PrefetchScalarGridSpec(
        num_scalar_prefetch=5,
        grid=(blocks,),
        in_specs=[pl.BlockSpec((1, 1, width, width), lambda i, *_: (i // top, i % top, 0, 0))] + [any_spec] * 10,
        out_specs=pl.BlockSpec((1, 1, width, width), lambda i, *_: (i // top, i % top, 0, 0)),
        scratch_shapes=[pltpu.VMEM((2, width, width), jnp.float32), pltpu.SemaphoreType.DMA((2, 2, 2))],
    )
    return pl.pallas_call(
        pick_kernel,
        grid_spec=grid_spec,
        out_shape=jax.ShapeDtypeStruct(theta.shape, jnp.float32),
        compiler_params=pltpu.CompilerParams(dimension_semantics=("arbitrary",)),
        cost_estimate=pl.CostEstimate(
            flops=6 * blocks * width ** 3, transcendentals=0, bytes_accessed=3 * 4 * blocks * width * width
        ),
    )(sel_a, sub_a, sel_b, sub_b, weight, theta, *pieces_a, *pieces_b)


def shards(theta, left_env, right_env, coeffs, live_states, dest_device, dest_local):
    sec_dev, top, width = theta.shape[0], theta.shape[1], theta.shape[2]
    me_sec = lax.axis_index("sec")
    mine = right_env[0]
    cut = width // 2
    held = right_env.shape[1]
    flat = lambda piece: piece.reshape(-1, piece.shape[-2], piece.shape[-1])
    pieces_a = [flat(p) for p in ring_gather(ring_stack(mine[..., :cut], 0), 1)]
    pieces_b = [flat(p) for p in ring_gather(ring_stack(mine[..., cut:], 1), 0)]
    dev_mine = lax.dynamic_slice_in_dim(dest_device[:, :, 0], me_sec * sec_dev, sec_dev, 0)
    local_mine = lax.dynamic_slice_in_dim(dest_local, me_sec * sec_dev, sec_dev, 0)
    live_mine = lax.dynamic_slice_in_dim(live_states, me_sec * sec_dev, sec_dev, 0)
    rel_x = ((dev_mine // SIDE - me_sec // SIDE) % SIDE).reshape(-1)
    rel_y = ((dev_mine % SIDE - me_sec % SIDE) % SIDE).reshape(-1)
    local_flat = local_mine.reshape(-1)
    weight = jnp.take(coeffs[0], live_mine, axis=0).reshape(-1)
    lefts_t = jnp.swapaxes(left_env[0], 1, 2)
    mixed = jnp.einsum("pca,pjab->pjcb", lefts_t, theta, precision=lax.Precision.HIGH)
    part = pick_product(
        mixed, weight,
        rel_y, rel_x * held + local_flat, pieces_a,
        rel_x, rel_y * held + local_flat, pieces_b,
    )
    return mpo_total(part)


def mpo_total(part):
    sec_dev, top, width = part.shape[0], part.shape[1], part.shape[2]
    planes = lax.axis_size("z")
    cores = lax.axis_size("core")
    rows = width // (planes * cores)
    grouped = part.reshape(sec_dev, top, planes, cores, rows, width)
    core = lax.axis_index("core")
    other = lax.dynamic_index_in_dim(grouped, 1 - core, 3, keepdims=False)
    keep = lax.dynamic_index_in_dim(grouped, core, 3, keepdims=False)
    arrived = lax.ppermute(other, "core", [(0, 1), (1, 0)])
    summed = keep + arrived
    total = lax.psum_scatter(summed, "z", scatter_dimension=2, tiled=True)
    return total.reshape(sec_dev, top, rows, width)


def solution(mesh):
    sec_size, mpo_size = mesh.devices.shape
    split = jax.sharding.Mesh(mesh.devices.reshape(sec_size, mpo_size // 2, 2), ("sec", "z", "core"))
    mpo = ("z", "core")
    return jax.shard_map(
        shards,
        mesh=split,
        in_specs=(
            P("sec", None, None, None),
            P(mpo, "sec", None, None),
            P(mpo, "sec", None, None),
            P(mpo, None),
            P(),
            P(),
            P(),
        ),
        out_specs=P("sec", None, mpo, None),
        check_vma=False,
    )
```

```python
import jax
import jax.numpy as jnp
from jax import lax
from jax.sharding import PartitionSpec as P
from jax.experimental import pallas as pl
from jax.experimental.pallas import tpu as pltpu

SIDE = 4


def torus_shift(axis, delta):
    pairs = []
    for x in range(SIDE):
        for y in range(SIDE):
            if axis == 0:
                pairs.append((x * SIDE + y, ((x + delta) % SIDE) * SIDE + y))
            else:
                pairs.append((x * SIDE + y, x * SIDE + (y + delta) % SIDE))
    return pairs


def ring_gather(block, axis):
    from_minus = lax.ppermute(block, "sec", torus_shift(axis, 1))
    from_plus = lax.ppermute(block, "sec", torus_shift(axis, -1))
    half = block.shape[-2] // 2
    far_low = lax.ppermute(from_minus[..., :half, :], "sec", torus_shift(axis, 1))
    far_high = lax.ppermute(from_plus[..., half:, :], "sec", torus_shift(axis, -1))
    return block, from_plus, far_low, far_high, from_minus


def ring_stack(block, axis):
    own, plus, far_low, far_high, minus = ring_gather(block, axis)
    return jnp.stack([own, plus, jnp.concatenate([far_low, far_high], axis=-2), minus])


def split_dot(a, b):
    a_high = a.astype(jnp.bfloat16)
    a_low = (a - a_high.astype(jnp.float32)).astype(jnp.bfloat16)
    b_high = b.astype(jnp.bfloat16)
    b_low = (b - b_high.astype(jnp.float32)).astype(jnp.bfloat16)
    dot = lambda x, y: jnp.dot(x, y, preferred_element_type=jnp.float32)
    return (dot(a_low, b_high) + dot(a_high, b_low)) + dot(a_high, b_high)


def pick_kernel(sel_a, sub_a, sel_b, sub_b, weight, mixed, a0, a1, a2, a3, a4, b0, b1, b2, b3, b4, out, held, sems):
    step = pl.program_id(0)
    steps = pl.num_programs(0)
    rows, cols = a0.shape[1], a0.shape[2]
    half = a2.shape[1]
    sides = ((sel_a, sub_a, (a0, a1, a2, a3, a4)), (sel_b, sub_b, (b0, b1, b2, b3, b4)))

    def fetch(index, slot, wait):
        for side, (sel, sub, pieces) in enumerate(sides):
            own, plus, low, high, minus = pieces
            case, k = sel[index], sub[index]
            whole = held.at[side, slot]
            top = held.at[side, slot, pl.ds(0, half)]
            bottom = held.at[side, slot, pl.ds(half, rows - half)]
            for number, src in ((0, own), (1, plus), (3, minus)):
                @pl.when(case == number)
                def _():
                    copy = pltpu.make_async_copy(src.at[k], whole, sems.at[slot, side, 0])
                    copy.wait() if wait else copy.start()

            @pl.when(case == 2)
            def _():
                first = pltpu.make_async_copy(low.at[k], top, sems.at[slot, side, 0])
                second = pltpu.make_async_copy(high.at[k], bottom, sems.at[slot, side, 1])
                if wait:
                    first.wait()
                    second.wait()
                else:
                    first.start()
                    second.start()

    slot = step % 2

    @pl.when(step == 0)
    def _():
        fetch(0, 0, False)

    @pl.when(step + 1 < steps)
    def _():
        fetch(step + 1, 1 - slot, False)

    fetch(step, slot, True)
    left = mixed[0, 0]
    scale = weight[step]
    out[0, 0, :, pl.ds(0, cols)] = split_dot(left, held[0, slot]) * scale
    out[0, 0, :, pl.ds(cols, cols)] = split_dot(left, held[1, slot]) * scale


def pick_product(theta, weight, sel_a, sub_a, pieces_a, sel_b, sub_b, pieces_b):
    sec_dev, top, width = theta.shape[0], theta.shape[1], theta.shape[2]
    blocks = sec_dev * top
    any_spec = pl.BlockSpec(memory_space=pl.ANY)
    grid_spec = pltpu.PrefetchScalarGridSpec(
        num_scalar_prefetch=5,
        grid=(blocks,),
        in_specs=[pl.BlockSpec((1, 1, width, width), lambda i, *_: (i // top, i % top, 0, 0))] + [any_spec] * 10,
        out_specs=pl.BlockSpec((1, 1, width, width), lambda i, *_: (i // top, i % top, 0, 0)),
        scratch_shapes=[pltpu.VMEM((2, 2, width, width // 2), jnp.float32), pltpu.SemaphoreType.DMA((2, 2, 2))],
    )
    return pl.pallas_call(
        pick_kernel,
        grid_spec=grid_spec,
        out_shape=jax.ShapeDtypeStruct(theta.shape, jnp.float32),
        compiler_params=pltpu.CompilerParams(dimension_semantics=("arbitrary",)),
        cost_estimate=pl.CostEstimate(
            flops=6 * blocks * width ** 3, transcendentals=0, bytes_accessed=3 * 4 * blocks * width * width
        ),
    )(sel_a, sub_a, sel_b, sub_b, weight, theta, *pieces_a, *pieces_b)


def shards(theta, left_env, right_env, coeffs, live_states, dest_device, dest_local):
    sec_dev, top, width = theta.shape[0], theta.shape[1], theta.shape[2]
    me_sec = lax.axis_index("sec")
    mine = right_env[0]
    cut = width // 2
    held = right_env.shape[1]
    flat = lambda piece: piece.reshape(-1, piece.shape[-2], piece.shape[-1])
    pieces_a = [flat(p) for p in ring_gather(ring_stack(mine[..., :cut], 0), 1)]
    pieces_b = [flat(p) for p in ring_gather(ring_stack(mine[..., cut:], 1), 0)]
    dev_mine = lax.dynamic_slice_in_dim(dest_device[:, :, 0], me_sec * sec_dev, sec_dev, 0)
    local_mine = lax.dynamic_slice_in_dim(dest_local, me_sec * sec_dev, sec_dev, 0)
    live_mine = lax.dynamic_slice_in_dim(live_states, me_sec * sec_dev, sec_dev, 0)
    rel_x = ((dev_mine // SIDE - me_sec // SIDE) % SIDE).reshape(-1)
    rel_y = ((dev_mine % SIDE - me_sec % SIDE) % SIDE).reshape(-1)
    local_flat = local_mine.reshape(-1)
    weight = jnp.take(coeffs[0], live_mine, axis=0).reshape(-1)
    lefts_t = jnp.swapaxes(left_env[0], 1, 2)
    mixed = jnp.einsum("pca,pjab->pjcb", lefts_t, theta, precision=lax.Precision.HIGH)
    part = pick_product(
        mixed, weight,
        rel_y, rel_x * held + local_flat, pieces_a,
        rel_x, rel_y * held + local_flat, pieces_b,
    )
    return mpo_total(part)


def mpo_total(part):
    sec_dev, top, width = part.shape[0], part.shape[1], part.shape[2]
    planes = lax.axis_size("z")
    cores = lax.axis_size("core")
    rows = width // (planes * cores)
    grouped = part.reshape(sec_dev, top, planes, cores, rows, width)
    core = lax.axis_index("core")
    other = lax.dynamic_index_in_dim(grouped, 1 - core, 3, keepdims=False)
    keep = lax.dynamic_index_in_dim(grouped, core, 3, keepdims=False)
    arrived = lax.ppermute(other, "core", [(0, 1), (1, 0)])
    summed = keep + arrived
    total = lax.psum_scatter(summed, "z", scatter_dimension=2, tiled=True)
    return total.reshape(sec_dev, top, rows, width)


def solution(mesh):
    sec_size, mpo_size = mesh.devices.shape
    split = jax.sharding.Mesh(mesh.devices.reshape(sec_size, mpo_size // 2, 2), ("sec", "z", "core"))
    mpo = ("z", "core")
    return jax.shard_map(
        shards,
        mesh=split,
        in_specs=(
            P("sec", None, None, None),
            P(mpo, "sec", None, None),
            P(mpo, "sec", None, None),
            P(mpo, None),
            P(),
            P(),
            P(),
        ),
        out_specs=P("sec", None, mpo, None),
        check_vma=False,
    )
```

```python
import jax
import jax.numpy as jnp
from jax import lax
from jax.sharding import PartitionSpec as P
from jax.experimental import pallas as pl
from jax.experimental.pallas import tpu as pltpu

SIDE = 4


def torus_shift(axis, delta):
    pairs = []
    for x in range(SIDE):
        for y in range(SIDE):
            if axis == 0:
                pairs.append((x * SIDE + y, ((x + delta) % SIDE) * SIDE + y))
            else:
                pairs.append((x * SIDE + y, x * SIDE + (y + delta) % SIDE))
    return pairs


def ring_gather(block, axis):
    from_minus = lax.ppermute(block, "sec", torus_shift(axis, 1))
    from_plus = lax.ppermute(block, "sec", torus_shift(axis, -1))
    half = block.shape[-2] // 2
    far_low = lax.ppermute(from_minus[..., :half, :], "sec", torus_shift(axis, 1))
    far_high = lax.ppermute(from_plus[..., half:, :], "sec", torus_shift(axis, -1))
    return block, from_plus, far_low, far_high, from_minus


def ring_stack(block, axis):
    own, plus, far_low, far_high, minus = ring_gather(block, axis)
    return jnp.stack([own, plus, jnp.concatenate([far_low, far_high], axis=-2), minus])


def split_dot(a, b):
    a_high = a.astype(jnp.bfloat16)
    a_low = (a - a_high.astype(jnp.float32)).astype(jnp.bfloat16)
    b_high = b.astype(jnp.bfloat16)
    b_low = (b - b_high.astype(jnp.float32)).astype(jnp.bfloat16)
    dot = lambda x, y: jnp.dot(x, y, preferred_element_type=jnp.float32)
    return (dot(a_low, b_high) + dot(a_high, b_low)) + dot(a_high, b_high)


GROUP = 4


def pick_kernel(sel_a, sub_a, sel_b, sub_b, weight, mixed, a0, a1, a2, a3, a4, b0, b1, b2, b3, b4, out, held, sems):
    step = pl.program_id(0)
    steps = pl.num_programs(0)
    rows, cols = a0.shape[1], a0.shape[2]
    half = a2.shape[1]
    sides = ((sel_a, sub_a, (a0, a1, a2, a3, a4)), (sel_b, sub_b, (b0, b1, b2, b3, b4)))

    def fetch(group, slot, wait):
        for member in range(GROUP):
            index = group * GROUP + member
            for side, (sel, sub, pieces) in enumerate(sides):
                own, plus, low, high, minus = pieces
                case, k = sel[index], sub[index]
                whole = held.at[side, slot, member]
                top = held.at[side, slot, member, pl.ds(0, half)]
                bottom = held.at[side, slot, member, pl.ds(half, rows - half)]
                sem_low = sems.at[slot, member, side, 0]
                sem_high = sems.at[slot, member, side, 1]
                for number, src in ((0, own), (1, plus), (3, minus)):
                    @pl.when(case == number)
                    def _():
                        copy = pltpu.make_async_copy(src.at[k], whole, sem_low)
                        copy.wait() if wait else copy.start()

                @pl.when(case == 2)
                def _():
                    first = pltpu.make_async_copy(low.at[k], top, sem_low)
                    second = pltpu.make_async_copy(high.at[k], bottom, sem_high)
                    if wait:
                        first.wait()
                        second.wait()
                    else:
                        first.start()
                        second.start()

    slot = step % 2

    @pl.when(step == 0)
    def _():
        fetch(0, 0, False)

    @pl.when(step + 1 < steps)
    def _():
        fetch(step + 1, 1 - slot, False)

    fetch(step, slot, True)
    for member in range(GROUP):
        left = mixed[0, member]
        scale = weight[step * GROUP + member]
        out[0, member, :, pl.ds(0, cols)] = split_dot(left, held[0, slot, member]) * scale
        out[0, member, :, pl.ds(cols, cols)] = split_dot(left, held[1, slot, member]) * scale


def pick_product(theta, weight, sel_a, sub_a, pieces_a, sel_b, sub_b, pieces_b):
    sec_dev, top, width = theta.shape[0], theta.shape[1], theta.shape[2]
    blocks = sec_dev * top
    per = top // GROUP
    any_spec = pl.BlockSpec(memory_space=pl.ANY)
    grid_spec = pltpu.PrefetchScalarGridSpec(
        num_scalar_prefetch=5,
        grid=(blocks // GROUP,),
        in_specs=[pl.BlockSpec((1, GROUP, width, width), lambda i, *_: (i // per, i % per, 0, 0))] + [any_spec] * 10,
        out_specs=pl.BlockSpec((1, GROUP, width, width), lambda i, *_: (i // per, i % per, 0, 0)),
        scratch_shapes=[
            pltpu.VMEM((2, 2, GROUP, width, width // 2), jnp.float32),
            pltpu.SemaphoreType.DMA((2, GROUP, 2, 2)),
        ],
    )
    return pl.pallas_call(
        pick_kernel,
        grid_spec=grid_spec,
        out_shape=jax.ShapeDtypeStruct(theta.shape, jnp.float32),
        compiler_params=pltpu.CompilerParams(dimension_semantics=("arbitrary",), vmem_limit_bytes=48 * 1024 * 1024),
        cost_estimate=pl.CostEstimate(
            flops=6 * blocks * width ** 3, transcendentals=0, bytes_accessed=3 * 4 * blocks * width * width
        ),
    )(sel_a, sub_a, sel_b, sub_b, weight, theta, *pieces_a, *pieces_b)


def shards(theta, left_env, right_env, coeffs, live_states, dest_device, dest_local):
    sec_dev, top, width = theta.shape[0], theta.shape[1], theta.shape[2]
    me_sec = lax.axis_index("sec")
    mine = right_env[0]
    cut = width // 2
    held = right_env.shape[1]
    flat = lambda piece: piece.reshape(-1, piece.shape[-2], piece.shape[-1])
    pieces_a = [flat(p) for p in ring_gather(ring_stack(mine[..., :cut], 0), 1)]
    pieces_b = [flat(p) for p in ring_gather(ring_stack(mine[..., cut:], 1), 0)]
    dev_mine = lax.dynamic_slice_in_dim(dest_device[:, :, 0], me_sec * sec_dev, sec_dev, 0)
    local_mine = lax.dynamic_slice_in_dim(dest_local, me_sec * sec_dev, sec_dev, 0)
    live_mine = lax.dynamic_slice_in_dim(live_states, me_sec * sec_dev, sec_dev, 0)
    rel_x = ((dev_mine // SIDE - me_sec // SIDE) % SIDE).reshape(-1)
    rel_y = ((dev_mine % SIDE - me_sec % SIDE) % SIDE).reshape(-1)
    local_flat = local_mine.reshape(-1)
    weight = jnp.take(coeffs[0], live_mine, axis=0).reshape(-1)
    lefts_t = jnp.swapaxes(left_env[0], 1, 2)
    mixed = jnp.einsum("pca,pjab->pjcb", lefts_t, theta, precision=lax.Precision.HIGH)
    part = pick_product(
        mixed, weight,
        rel_y, rel_x * held + local_flat, pieces_a,
        rel_x, rel_y * held + local_flat, pieces_b,
    )
    return mpo_total(part)


def mpo_total(part):
    sec_dev, top, width = part.shape[0], part.shape[1], part.shape[2]
    planes = lax.axis_size("z")
    cores = lax.axis_size("core")
    rows = width // (planes * cores)
    grouped = part.reshape(sec_dev, top, planes, cores, rows, width)
    core = lax.axis_index("core")
    other = lax.dynamic_index_in_dim(grouped, 1 - core, 3, keepdims=False)
    keep = lax.dynamic_index_in_dim(grouped, core, 3, keepdims=False)
    arrived = lax.ppermute(other, "core", [(0, 1), (1, 0)])
    summed = keep + arrived
    total = lax.psum_scatter(summed, "z", scatter_dimension=2, tiled=True)
    return total.reshape(sec_dev, top, rows, width)


def solution(mesh):
    sec_size, mpo_size = mesh.devices.shape
    split = jax.sharding.Mesh(mesh.devices.reshape(sec_size, mpo_size // 2, 2), ("sec", "z", "core"))
    mpo = ("z", "core")
    return jax.shard_map(
        shards,
        mesh=split,
        in_specs=(
            P("sec", None, None, None),
            P(mpo, "sec", None, None),
            P(mpo, "sec", None, None),
            P(mpo, None),
            P(),
            P(),
            P(),
        ),
        out_specs=P("sec", None, mpo, None),
        check_vma=False,
    )
```

```python
import jax
import jax.numpy as jnp
from jax import lax
from jax.sharding import PartitionSpec as P
from jax.experimental import pallas as pl
from jax.experimental.pallas import tpu as pltpu

SIDE = 4


def torus_shift(axis, delta):
    pairs = []
    for x in range(SIDE):
        for y in range(SIDE):
            if axis == 0:
                pairs.append((x * SIDE + y, ((x + delta) % SIDE) * SIDE + y))
            else:
                pairs.append((x * SIDE + y, x * SIDE + (y + delta) % SIDE))
    return pairs


def ring_gather(block, axis):
    from_minus = lax.ppermute(block, "sec", torus_shift(axis, 1))
    from_plus = lax.ppermute(block, "sec", torus_shift(axis, -1))
    half = block.shape[-2] // 2
    far_low = lax.ppermute(from_minus[..., :half, :], "sec", torus_shift(axis, 1))
    far_high = lax.ppermute(from_plus[..., half:, :], "sec", torus_shift(axis, -1))
    return block, from_plus, far_low, far_high, from_minus


def ring_stack(block, axis):
    own, plus, far_low, far_high, minus = ring_gather(block, axis)
    return jnp.stack([own, plus, jnp.concatenate([far_low, far_high], axis=-2), minus])


def split_dot(a, b):
    a_high = a.astype(jnp.bfloat16)
    a_low = (a - a_high.astype(jnp.float32)).astype(jnp.bfloat16)
    b_high = b.astype(jnp.bfloat16)
    b_low = (b - b_high.astype(jnp.float32)).astype(jnp.bfloat16)
    dot = lambda x, y: jnp.dot(x, y, preferred_element_type=jnp.float32)
    return (dot(a_low, b_high) + dot(a_high, b_low)) + dot(a_high, b_high)


GROUP = 8


def pick_kernel(sel_a, sub_a, sel_b, sub_b, weight, core, mixed, a0, a1, a2, a3, a4, b0, b1, b2, b3, b4, keep, send, held, sems, prod):
    step = pl.program_id(0)
    steps = pl.num_programs(0)
    rows, cols = a0.shape[1], a0.shape[2]
    half = a2.shape[1]
    sides = ((sel_a, sub_a, (a0, a1, a2, a3, a4)), (sel_b, sub_b, (b0, b1, b2, b3, b4)))

    def fetch(group, slot, wait):
        for member in range(GROUP):
            index = group * GROUP + member
            for side, (sel, sub, pieces) in enumerate(sides):
                own, plus, low, high, minus = pieces
                case, k = sel[index], sub[index]
                whole = held.at[side, slot, member]
                top = held.at[side, slot, member, pl.ds(0, half)]
                bottom = held.at[side, slot, member, pl.ds(half, rows - half)]
                sem_low = sems.at[slot, member, side, 0]
                sem_high = sems.at[slot, member, side, 1]
                for number, src in ((0, own), (1, plus), (3, minus)):
                    @pl.when(case == number)
                    def _():
                        copy = pltpu.make_async_copy(src.at[k], whole, sem_low)
                        copy.wait() if wait else copy.start()

                @pl.when(case == 2)
                def _():
                    first = pltpu.make_async_copy(low.at[k], top, sem_low)
                    second = pltpu.make_async_copy(high.at[k], bottom, sem_high)
                    if wait:
                        first.wait()
                        second.wait()
                    else:
                        first.start()
                        second.start()

    slot = step % 2

    @pl.when(step == 0)
    def _():
        fetch(0, 0, False)

    @pl.when(step + 1 < steps)
    def _():
        fetch(step + 1, 1 - slot, False)

    fetch(step, slot, True)
    planes, strip = keep.shape[0], keep.shape[2]
    mine = core[0]
    for member in range(GROUP):
        left = mixed[0, member]
        scale = weight[step * GROUP + member]
        prod[:, pl.ds(0, cols)] = split_dot(left, held[0, slot, member]) * scale
        prod[:, pl.ds(cols, cols)] = split_dot(left, held[1, slot, member]) * scale
        for plane in range(planes):
            keep[plane, member] = prod[pl.ds(pl.multiple_of((plane * 2 + mine) * strip, strip), strip), :]
            send[plane, member] = prod[pl.ds(pl.multiple_of((plane * 2 + 1 - mine) * strip, strip), strip), :]


def pick_product(theta, weight, core, planes, sel_a, sub_a, pieces_a, sel_b, sub_b, pieces_b):
    sec_dev, top, width = theta.shape[0], theta.shape[1], theta.shape[2]
    blocks = sec_dev * top
    per = top // GROUP
    strip = width // (2 * planes)
    any_spec = pl.BlockSpec(memory_space=pl.ANY)
    half_spec = pl.BlockSpec((planes, GROUP, strip, width), lambda i, *_: (0, i, 0, 0))
    grid_spec = pltpu.PrefetchScalarGridSpec(
        num_scalar_prefetch=6,
        grid=(blocks // GROUP,),
        in_specs=[pl.BlockSpec((1, GROUP, width, width), lambda i, *_: (i // per, i % per, 0, 0))] + [any_spec] * 10,
        out_specs=[half_spec, half_spec],
        scratch_shapes=[
            pltpu.VMEM((2, 2, GROUP, width, width // 2), jnp.float32),
            pltpu.SemaphoreType.DMA((2, GROUP, 2, 2)),
            pltpu.VMEM((width, width), jnp.float32),
        ],
    )
    half_shape = jax.ShapeDtypeStruct((planes, blocks, strip, width), jnp.float32)
    return pl.pallas_call(
        pick_kernel,
        grid_spec=grid_spec,
        out_shape=[half_shape, half_shape],
        compiler_params=pltpu.CompilerParams(dimension_semantics=("arbitrary",), vmem_limit_bytes=48 * 1024 * 1024),
        cost_estimate=pl.CostEstimate(
            flops=6 * blocks * width ** 3, transcendentals=0, bytes_accessed=3 * 4 * blocks * width * width
        ),
    )(sel_a, sub_a, sel_b, sub_b, weight, core, theta, *pieces_a, *pieces_b)


def shards(theta, left_env, right_env, coeffs, live_states, dest_device, dest_local):
    sec_dev, top, width = theta.shape[0], theta.shape[1], theta.shape[2]
    me_sec = lax.axis_index("sec")
    mine = right_env[0]
    cut = width // 2
    held = right_env.shape[1]
    flat = lambda piece: piece.reshape(-1, piece.shape[-2], piece.shape[-1])
    pieces_a = [flat(p) for p in ring_gather(ring_stack(mine[..., :cut], 0), 1)]
    pieces_b = [flat(p) for p in ring_gather(ring_stack(mine[..., cut:], 1), 0)]
    dev_mine = lax.dynamic_slice_in_dim(dest_device[:, :, 0], me_sec * sec_dev, sec_dev, 0)
    local_mine = lax.dynamic_slice_in_dim(dest_local, me_sec * sec_dev, sec_dev, 0)
    live_mine = lax.dynamic_slice_in_dim(live_states, me_sec * sec_dev, sec_dev, 0)
    rel_x = ((dev_mine // SIDE - me_sec // SIDE) % SIDE).reshape(-1)
    rel_y = ((dev_mine % SIDE - me_sec % SIDE) % SIDE).reshape(-1)
    local_flat = local_mine.reshape(-1)
    weight = jnp.take(coeffs[0], live_mine, axis=0).reshape(-1)
    lefts_t = jnp.swapaxes(left_env[0], 1, 2)
    mixed = jnp.einsum("pca,pjab->pjcb", lefts_t, theta, precision=lax.Precision.HIGH)
    core = lax.axis_index("core").astype(jnp.int32).reshape(1)
    planes = lax.axis_size("z")
    keep, send = pick_product(
        mixed, weight, core, planes,
        rel_y, rel_x * held + local_flat, pieces_a,
        rel_x, rel_y * held + local_flat, pieces_b,
    )
    arrived = lax.ppermute(send, "core", [(0, 1), (1, 0)])
    total = lax.psum_scatter(keep + arrived, "z", scatter_dimension=0, tiled=True)
    return total.reshape(sec_dev, top, width // (2 * planes), width)


def solution(mesh):
    sec_size, mpo_size = mesh.devices.shape
    split = jax.sharding.Mesh(mesh.devices.reshape(sec_size, mpo_size // 2, 2), ("sec", "z", "core"))
    mpo = ("z", "core")
    return jax.shard_map(
        shards,
        mesh=split,
        in_specs=(
            P("sec", None, None, None),
            P(mpo, "sec", None, None),
            P(mpo, "sec", None, None),
            P(mpo, None),
            P(),
            P(),
            P(),
        ),
        out_specs=P("sec", None, mpo, None),
        check_vma=False,
    )
```

```python
import jax
import jax.numpy as jnp
from jax import lax
from jax.sharding import PartitionSpec as P
from jax.experimental import pallas as pl
from jax.experimental.pallas import tpu as pltpu

SIDE = 4


def torus_shift(axis, delta):
    pairs = []
    for x in range(SIDE):
        for y in range(SIDE):
            if axis == 0:
                pairs.append((x * SIDE + y, ((x + delta) % SIDE) * SIDE + y))
            else:
                pairs.append((x * SIDE + y, x * SIDE + (y + delta) % SIDE))
    return pairs


def ring_gather(block, axis):
    from_minus = lax.ppermute(block, "sec", torus_shift(axis, 1))
    from_plus = lax.ppermute(block, "sec", torus_shift(axis, -1))
    half = block.shape[-2] // 2
    far_low = lax.ppermute(from_minus[..., :half, :], "sec", torus_shift(axis, 1))
    far_high = lax.ppermute(from_plus[..., half:, :], "sec", torus_shift(axis, -1))
    return block, from_plus, far_low, far_high, from_minus


def ring_stack(block, axis):
    from_minus = lax.ppermute(block, "sec", torus_shift(axis, 1))
    from_plus = lax.ppermute(block, "sec", torus_shift(axis, -1))
    far = lax.ppermute(from_minus, "sec", torus_shift(axis, 1))
    return jnp.stack([block, from_plus, far, from_minus])


def split_dot(a, b):
    a_high = a.astype(jnp.bfloat16)
    a_low = (a - a_high.astype(jnp.float32)).astype(jnp.bfloat16)
    b_high = b.astype(jnp.bfloat16)
    b_low = (b - b_high.astype(jnp.float32)).astype(jnp.bfloat16)
    dot = lambda x, y: jnp.dot(x, y, preferred_element_type=jnp.float32)
    return (dot(a_low, b_high) + dot(a_high, b_low)) + dot(a_high, b_high)


GROUP = 4


def pick_kernel(sel_a, sub_a, sel_b, sub_b, weight, mixed, a0, a1, a2, a3, a4, b0, b1, b2, b3, b4, out, held, sems):
    step = pl.program_id(0)
    steps = pl.num_programs(0)
    rows, cols = a0.shape[1], a0.shape[2]
    half = a2.shape[1]
    sides = ((sel_a, sub_a, (a0, a1, a2, a3, a4)), (sel_b, sub_b, (b0, b1, b2, b3, b4)))

    def fetch(group, slot, wait):
        for member in range(GROUP):
            index = group * GROUP + member
            for side, (sel, sub, pieces) in enumerate(sides):
                own, plus, low, high, minus = pieces
                case, k = sel[index], sub[index]
                whole = held.at[side, slot, member]
                top = held.at[side, slot, member, pl.ds(0, half)]
                bottom = held.at[side, slot, member, pl.ds(half, rows - half)]
                sem_low = sems.at[slot, member, side, 0]
                sem_high = sems.at[slot, member, side, 1]
                for number, src in ((0, own), (1, plus), (3, minus)):
                    @pl.when(case == number)
                    def _():
                        copy = pltpu.make_async_copy(src.at[k], whole, sem_low)
                        copy.wait() if wait else copy.start()

                @pl.when(case == 2)
                def _():
                    first = pltpu.make_async_copy(low.at[k], top, sem_low)
                    second = pltpu.make_async_copy(high.at[k], bottom, sem_high)
                    if wait:
                        first.wait()
                        second.wait()
                    else:
                        first.start()
                        second.start()

    slot = step % 2

    @pl.when(step == 0)
    def _():
        fetch(0, 0, False)

    @pl.when(step + 1 < steps)
    def _():
        fetch(step + 1, 1 - slot, False)

    fetch(step, slot, True)
    for member in range(GROUP):
        left = mixed[0, member]
        scale = weight[step * GROUP + member]
        out[0, member, :, pl.ds(0, cols)] = split_dot(left, held[0, slot, member]) * scale
        out[0, member, :, pl.ds(cols, cols)] = split_dot(left, held[1, slot, member]) * scale


def pick_product(theta, weight, sel_a, sub_a, pieces_a, sel_b, sub_b, pieces_b):
    sec_dev, top, width = theta.shape[0], theta.shape[1], theta.shape[2]
    blocks = sec_dev * top
    per = top // GROUP
    any_spec = pl.BlockSpec(memory_space=pl.ANY)
    grid_spec = pltpu.PrefetchScalarGridSpec(
        num_scalar_prefetch=5,
        grid=(blocks // GROUP,),
        in_specs=[pl.BlockSpec((1, GROUP, width, width), lambda i, *_: (i // per, i % per, 0, 0))] + [any_spec] * 10,
        out_specs=pl.BlockSpec((1, GROUP, width, width), lambda i, *_: (i // per, i % per, 0, 0)),
        scratch_shapes=[
            pltpu.VMEM((2, 2, GROUP, width, width // 2), jnp.float32),
            pltpu.SemaphoreType.DMA((2, GROUP, 2, 2)),
        ],
    )
    return pl.pallas_call(
        pick_kernel,
        grid_spec=grid_spec,
        out_shape=jax.ShapeDtypeStruct(theta.shape, jnp.float32),
        compiler_params=pltpu.CompilerParams(dimension_semantics=("arbitrary",), vmem_limit_bytes=48 * 1024 * 1024),
        cost_estimate=pl.CostEstimate(
            flops=6 * blocks * width ** 3, transcendentals=0, bytes_accessed=3 * 4 * blocks * width * width
        ),
    )(sel_a, sub_a, sel_b, sub_b, weight, theta, *pieces_a, *pieces_b)


def shards(theta, left_env, right_env, coeffs, live_states, dest_device, dest_local):
    sec_dev, top, width = theta.shape[0], theta.shape[1], theta.shape[2]
    me_sec = lax.axis_index("sec")
    mine = right_env[0]
    cut = width // 2
    held = right_env.shape[1]
    flat = lambda piece: piece.reshape(-1, piece.shape[-2], piece.shape[-1])
    pieces_a = [flat(p) for p in ring_gather(ring_stack(mine[..., :cut], 0), 1)]
    pieces_b = [flat(p) for p in ring_gather(ring_stack(mine[..., cut:], 1), 0)]
    dev_mine = lax.dynamic_slice_in_dim(dest_device[:, :, 0], me_sec * sec_dev, sec_dev, 0)
    local_mine = lax.dynamic_slice_in_dim(dest_local, me_sec * sec_dev, sec_dev, 0)
    live_mine = lax.dynamic_slice_in_dim(live_states, me_sec * sec_dev, sec_dev, 0)
    rel_x = ((dev_mine // SIDE - me_sec // SIDE) % SIDE).reshape(-1)
    rel_y = ((dev_mine % SIDE - me_sec % SIDE) % SIDE).reshape(-1)
    local_flat = local_mine.reshape(-1)
    weight = jnp.take(coeffs[0], live_mine, axis=0).reshape(-1)
    lefts_t = jnp.swapaxes(left_env[0], 1, 2)
    mixed = jnp.einsum("pca,pjab->pjcb", lefts_t, theta, precision=lax.Precision.HIGH)
    part = pick_product(
        mixed, weight,
        rel_y, rel_x * held + local_flat, pieces_a,
        rel_x, rel_y * held + local_flat, pieces_b,
    )
    return mpo_total(part)


def mpo_total(part):
    sec_dev, top, width = part.shape[0], part.shape[1], part.shape[2]
    planes = lax.axis_size("z")
    cores = lax.axis_size("core")
    rows = width // (planes * cores)
    grouped = part.reshape(sec_dev, top, planes, cores, rows, width)
    core = lax.axis_index("core")
    other = lax.dynamic_index_in_dim(grouped, 1 - core, 3, keepdims=False)
    keep = lax.dynamic_index_in_dim(grouped, core, 3, keepdims=False)
    arrived = lax.ppermute(other, "core", [(0, 1), (1, 0)])
    summed = keep + arrived
    total = lax.psum_scatter(summed, "z", scatter_dimension=2, tiled=True)
    return total.reshape(sec_dev, top, rows, width)


def solution(mesh):
    sec_size, mpo_size = mesh.devices.shape
    split = jax.sharding.Mesh(mesh.devices.reshape(sec_size, mpo_size // 2, 2), ("sec", "z", "core"))
    mpo = ("z", "core")
    return jax.shard_map(
        shards,
        mesh=split,
        in_specs=(
            P("sec", None, None, None),
            P(mpo, "sec", None, None),
            P(mpo, "sec", None, None),
            P(mpo, None),
            P(),
            P(),
            P(),
        ),
        out_specs=P("sec", None, mpo, None),
        check_vma=False,
    )
```

```python
import jax
import jax.numpy as jnp
from jax import lax
from jax.sharding import PartitionSpec as P
from jax.experimental import pallas as pl
from jax.experimental.pallas import tpu as pltpu

SIDE = 4


def torus_shift(axis, delta):
    pairs = []
    for x in range(SIDE):
        for y in range(SIDE):
            if axis == 0:
                pairs.append((x * SIDE + y, ((x + delta) % SIDE) * SIDE + y))
            else:
                pairs.append((x * SIDE + y, x * SIDE + (y + delta) % SIDE))
    return pairs


def ring_gather(block, axis):
    from_minus = lax.ppermute(block, "sec", torus_shift(axis, 1))
    from_plus = lax.ppermute(block, "sec", torus_shift(axis, -1))
    half = block.shape[-2] // 2
    far_low = lax.ppermute(from_minus[..., :half, :], "sec", torus_shift(axis, 1))
    far_high = lax.ppermute(from_plus[..., half:, :], "sec", torus_shift(axis, -1))
    return block, from_plus, far_low, far_high, from_minus


def ring_stack(block, axis):
    own, plus, far_low, far_high, minus = ring_gather(block, axis)
    return jnp.stack([own, plus, jnp.concatenate([far_low, far_high], axis=-2), minus])


def split_dot(a, b):
    a_high = a.astype(jnp.bfloat16)
    a_low = (a - a_high.astype(jnp.float32)).astype(jnp.bfloat16)
    b_high = b.astype(jnp.bfloat16)
    b_low = (b - b_high.astype(jnp.float32)).astype(jnp.bfloat16)
    dot = lambda x, y: jnp.dot(x, y, preferred_element_type=jnp.float32)
    return (dot(a_low, b_high) + dot(a_high, b_low)) + dot(a_high, b_high)


GROUP = 4


def pick_kernel(sel_a, sub_a, sel_b, sub_b, weight, mixed, a0, a1, a2, a3, a4, b0, b1, b2, b3, b4, out, held, sems):
    step = pl.program_id(0)
    steps = pl.num_programs(0)
    rows, cols = a0.shape[1], a0.shape[2]
    half = a2.shape[1]
    sides = ((sel_a, sub_a, (a0, a1, a2, a3, a4)), (sel_b, sub_b, (b0, b1, b2, b3, b4)))

    def fetch(group, slot, wait):
        for member in range(GROUP):
            index = group * GROUP + member
            for side, (sel, sub, pieces) in enumerate(sides):
                own, plus, low, high, minus = pieces
                case, k = sel[index], sub[index]
                whole = held.at[side, slot, member]
                top = held.at[side, slot, member, pl.ds(0, half)]
                bottom = held.at[side, slot, member, pl.ds(half, rows - half)]
                sem_low = sems.at[slot, member, side, 0]
                sem_high = sems.at[slot, member, side, 1]
                for number, src in ((0, own), (1, plus), (3, minus)):
                    @pl.when(case == number)
                    def _():
                        copy = pltpu.make_async_copy(src.at[k], whole, sem_low)
                        copy.wait() if wait else copy.start()

                @pl.when(case == 2)
                def _():
                    first = pltpu.make_async_copy(low.at[k], top, sem_low)
                    second = pltpu.make_async_copy(high.at[k], bottom, sem_high)
                    if wait:
                        first.wait()
                        second.wait()
                    else:
                        first.start()
                        second.start()

    slot = step % 2

    @pl.when(step == 0)
    def _():
        fetch(0, 0, False)

    @pl.when(step + 1 < steps)
    def _():
        fetch(step + 1, 1 - slot, False)

    fetch(step, slot, True)
    for member in range(GROUP):
        left = mixed[0, member]
        scale = weight[step * GROUP + member]
        out[0, member, :, pl.ds(0, cols)] = split_dot(left, held[0, slot, member]) * scale
        out[0, member, :, pl.ds(cols, cols)] = split_dot(left, held[1, slot, member]) * scale


def pick_product(theta, weight, sel_a, sub_a, pieces_a, sel_b, sub_b, pieces_b):
    sec_dev, top, width = theta.shape[0], theta.shape[1], theta.shape[2]
    blocks = sec_dev * top
    per = top // GROUP
    any_spec = pl.BlockSpec(memory_space=pl.ANY)
    grid_spec = pltpu.PrefetchScalarGridSpec(
        num_scalar_prefetch=5,
        grid=(blocks // GROUP,),
        in_specs=[pl.BlockSpec((1, GROUP, width, width), lambda i, *_: (i // per, i % per, 0, 0))] + [any_spec] * 10,
        out_specs=pl.BlockSpec((1, GROUP, width, width), lambda i, *_: (i // per, i % per, 0, 0)),
        scratch_shapes=[
            pltpu.VMEM((2, 2, GROUP, width, width // 2), jnp.float32),
            pltpu.SemaphoreType.DMA((2, GROUP, 2, 2)),
        ],
    )
    return pl.pallas_call(
        pick_kernel,
        grid_spec=grid_spec,
        out_shape=jax.ShapeDtypeStruct(theta.shape, jnp.float32),
        compiler_params=pltpu.CompilerParams(dimension_semantics=("arbitrary",), vmem_limit_bytes=48 * 1024 * 1024),
        cost_estimate=pl.CostEstimate(
            flops=6 * blocks * width ** 3, transcendentals=0, bytes_accessed=3 * 4 * blocks * width * width
        ),
    )(sel_a, sub_a, sel_b, sub_b, weight, theta, *pieces_a, *pieces_b)


def shards(theta, left_env, right_env, coeffs, live_states, dest_device, dest_local):
    sec_dev, top, width = theta.shape[0], theta.shape[1], theta.shape[2]
    me_sec = lax.axis_index("sec")
    mine = right_env[0]
    cut = width // 2
    held = right_env.shape[1]
    flat = lambda piece: piece.reshape(-1, piece.shape[-2], piece.shape[-1])
    pieces_a = [flat(p) for p in ring_gather(ring_stack(mine[..., :cut], 0), 1)]
    pieces_b = [flat(p) for p in ring_gather(ring_stack(mine[..., cut:], 1), 0)]
    dev_mine = lax.dynamic_slice_in_dim(dest_device[:, :, 0], me_sec * sec_dev, sec_dev, 0)
    local_mine = lax.dynamic_slice_in_dim(dest_local, me_sec * sec_dev, sec_dev, 0)
    live_mine = lax.dynamic_slice_in_dim(live_states, me_sec * sec_dev, sec_dev, 0)
    rel_x = ((dev_mine // SIDE - me_sec // SIDE) % SIDE).reshape(-1)
    rel_y = ((dev_mine % SIDE - me_sec % SIDE) % SIDE).reshape(-1)
    local_flat = local_mine.reshape(-1)
    weight = jnp.take(coeffs[0], live_mine, axis=0).reshape(-1)
    lefts_t = jnp.swapaxes(left_env[0], 1, 2)
    mixed = jnp.einsum("pca,pjab->pjcb", lefts_t, theta, precision=lax.Precision.HIGH)
    halves = []
    for p in range(sec_dev):
        rows_of = slice(p * top, (p + 1) * top)
        part = pick_product(
            mixed[p:p + 1], weight[rows_of],
            rel_y[rows_of], (rel_x * held + local_flat)[rows_of], pieces_a,
            rel_x[rows_of], (rel_y * held + local_flat)[rows_of], pieces_b,
        )
        halves.append(core_sum(part))
    return scatter_z(jnp.concatenate(halves, axis=0))


def core_sum(part):
    sec_dev, top, width = part.shape[0], part.shape[1], part.shape[2]
    planes = lax.axis_size("z")
    cores = lax.axis_size("core")
    rows = width // (planes * cores)
    grouped = part.reshape(sec_dev, top, planes, cores, rows, width)
    core = lax.axis_index("core")
    other = lax.dynamic_index_in_dim(grouped, 1 - core, 3, keepdims=False)
    keep = lax.dynamic_index_in_dim(grouped, core, 3, keepdims=False)
    arrived = lax.ppermute(other, "core", [(0, 1), (1, 0)])
    return keep + arrived


def scatter_z(summed):
    sec_dev, top, rows, width = summed.shape[0], summed.shape[1], summed.shape[3], summed.shape[4]
    total = lax.psum_scatter(summed, "z", scatter_dimension=2, tiled=True)
    return total.reshape(sec_dev, top, rows, width)


def solution(mesh):
    sec_size, mpo_size = mesh.devices.shape
    split = jax.sharding.Mesh(mesh.devices.reshape(sec_size, mpo_size // 2, 2), ("sec", "z", "core"))
    mpo = ("z", "core")
    return jax.shard_map(
        shards,
        mesh=split,
        in_specs=(
            P("sec", None, None, None),
            P(mpo, "sec", None, None),
            P(mpo, "sec", None, None),
            P(mpo, None),
            P(),
            P(),
            P(),
        ),
        out_specs=P("sec", None, mpo, None),
        check_vma=False,
    )
```

```python
import jax
import jax.numpy as jnp
from jax import lax
from jax.sharding import PartitionSpec as P
from jax.experimental import pallas as pl
from jax.experimental.pallas import tpu as pltpu

SIDE = 4


def torus_shift(axis, delta):
    pairs = []
    for x in range(SIDE):
        for y in range(SIDE):
            if axis == 0:
                pairs.append((x * SIDE + y, ((x + delta) % SIDE) * SIDE + y))
            else:
                pairs.append((x * SIDE + y, x * SIDE + (y + delta) % SIDE))
    return pairs


def ring_gather(block, axis):
    from_minus = lax.ppermute(block, "sec", torus_shift(axis, 1))
    from_plus = lax.ppermute(block, "sec", torus_shift(axis, -1))
    half = block.shape[-2] // 2
    far_low = lax.ppermute(from_minus[..., :half, :], "sec", torus_shift(axis, 1))
    far_high = lax.ppermute(from_plus[..., half:, :], "sec", torus_shift(axis, -1))
    return block, from_plus, far_low, far_high, from_minus


def ring_stack(block, axis):
    own, plus, far_low, far_high, minus = ring_gather(block, axis)
    return jnp.stack([own, plus, jnp.concatenate([far_low, far_high], axis=-2), minus])


def split_dot(a, b):
    a_high = a.astype(jnp.bfloat16)
    a_low = (a - a_high.astype(jnp.float32)).astype(jnp.bfloat16)
    b_high = b.astype(jnp.bfloat16)
    b_low = (b - b_high.astype(jnp.float32)).astype(jnp.bfloat16)
    dot = lambda x, y: jnp.dot(x, y, preferred_element_type=jnp.float32)
    return (dot(a_low, b_high) + dot(a_high, b_low)) + dot(a_high, b_high)


GROUP = 8


def pick_kernel(sel_a, sub_a, sel_b, sub_b, weight, mixed, a0, a1, a2, a3, a4, b0, b1, b2, b3, b4, out, held, sems):
    step = pl.program_id(0)
    steps = pl.num_programs(0)
    rows, cols = a0.shape[1], a0.shape[2]
    half = a2.shape[1]
    sides = ((sel_a, sub_a, (a0, a1, a2, a3, a4)), (sel_b, sub_b, (b0, b1, b2, b3, b4)))

    def fetch(group, slot, wait):
        for member in range(GROUP):
            index = group * GROUP + member
            for side, (sel, sub, pieces) in enumerate(sides):
                own, plus, low, high, minus = pieces
                case, k = sel[index], sub[index]
                whole = held.at[side, slot, member]
                top = held.at[side, slot, member, pl.ds(0, half)]
                bottom = held.at[side, slot, member, pl.ds(half, rows - half)]
                sem_low = sems.at[slot, member, side, 0]
                sem_high = sems.at[slot, member, side, 1]
                for number, src in ((0, own), (1, plus), (3, minus)):
                    @pl.when(case == number)
                    def _():
                        copy = pltpu.make_async_copy(src.at[k], whole, sem_low)
                        copy.wait() if wait else copy.start()

                @pl.when(case == 2)
                def _():
                    first = pltpu.make_async_copy(low.at[k], top, sem_low)
                    second = pltpu.make_async_copy(high.at[k], bottom, sem_high)
                    if wait:
                        first.wait()
                        second.wait()
                    else:
                        first.start()
                        second.start()

    slot = step % 2

    @pl.when(step == 0)
    def _():
        fetch(0, 0, False)

    @pl.when(step + 1 < steps)
    def _():
        fetch(step + 1, 1 - slot, False)

    fetch(step, slot, True)
    for member in range(GROUP):
        left = mixed[0, member]
        scale = weight[step * GROUP + member]
        out[0, member, :, pl.ds(0, cols)] = split_dot(left, held[0, slot, member]) * scale
        out[0, member, :, pl.ds(cols, cols)] = split_dot(left, held[1, slot, member]) * scale


def pick_product(theta, weight, sel_a, sub_a, pieces_a, sel_b, sub_b, pieces_b):
    sec_dev, top, width = theta.shape[0], theta.shape[1], theta.shape[2]
    blocks = sec_dev * top
    per = top // GROUP
    any_spec = pl.BlockSpec(memory_space=pl.ANY)
    grid_spec = pltpu.PrefetchScalarGridSpec(
        num_scalar_prefetch=5,
        grid=(blocks // GROUP,),
        in_specs=[pl.BlockSpec((1, GROUP, width, width), lambda i, *_: (i // per, i % per, 0, 0))] + [any_spec] * 10,
        out_specs=pl.BlockSpec((1, GROUP, width, width), lambda i, *_: (i // per, i % per, 0, 0)),
        scratch_shapes=[
            pltpu.VMEM((2, 2, GROUP, width, width // 2), jnp.float32),
            pltpu.SemaphoreType.DMA((2, GROUP, 2, 2)),
        ],
    )
    return pl.pallas_call(
        pick_kernel,
        grid_spec=grid_spec,
        out_shape=jax.ShapeDtypeStruct(theta.shape, jnp.float32),
        compiler_params=pltpu.CompilerParams(dimension_semantics=("arbitrary",), vmem_limit_bytes=48 * 1024 * 1024),
        cost_estimate=pl.CostEstimate(
            flops=6 * blocks * width ** 3, transcendentals=0, bytes_accessed=3 * 4 * blocks * width * width
        ),
    )(sel_a, sub_a, sel_b, sub_b, weight, theta, *pieces_a, *pieces_b)


def shards(theta, left_env, right_env, coeffs, live_states, dest_device, dest_local):
    sec_dev, top, width = theta.shape[0], theta.shape[1], theta.shape[2]
    me_sec = lax.axis_index("sec")
    mine = right_env[0]
    cut = width // 2
    held = right_env.shape[1]
    flat = lambda piece: piece.reshape(-1, piece.shape[-2], piece.shape[-1])
    pieces_a = [flat(p) for p in ring_gather(ring_stack(mine[..., :cut], 0), 1)]
    pieces_b = [flat(p) for p in ring_gather(ring_stack(mine[..., cut:], 1), 0)]
    dev_mine = lax.dynamic_slice_in_dim(dest_device[:, :, 0], me_sec * sec_dev, sec_dev, 0)
    local_mine = lax.dynamic_slice_in_dim(dest_local, me_sec * sec_dev, sec_dev, 0)
    live_mine = lax.dynamic_slice_in_dim(live_states, me_sec * sec_dev, sec_dev, 0)
    rel_x = ((dev_mine // SIDE - me_sec // SIDE) % SIDE).reshape(-1)
    rel_y = ((dev_mine % SIDE - me_sec % SIDE) % SIDE).reshape(-1)
    local_flat = local_mine.reshape(-1)
    weight = jnp.take(coeffs[0], live_mine, axis=0).reshape(-1)
    lefts_t = jnp.swapaxes(left_env[0], 1, 2)
    mixed = jnp.einsum("pca,pjab->pjcb", lefts_t, theta, precision=lax.Precision.HIGH)
    halves = []
    for p in range(sec_dev):
        rows_of = slice(p * top, (p + 1) * top)
        part = pick_product(
            mixed[p:p + 1], weight[rows_of],
            rel_y[rows_of], (rel_x * held + local_flat)[rows_of], pieces_a,
            rel_x[rows_of], (rel_y * held + local_flat)[rows_of], pieces_b,
        )
        halves.append(core_sum(part))
    return scatter_z(jnp.concatenate(halves, axis=0))


def core_sum(part):
    sec_dev, top, width = part.shape[0], part.shape[1], part.shape[2]
    planes = lax.axis_size("z")
    cores = lax.axis_size("core")
    rows = width // (planes * cores)
    grouped = part.reshape(sec_dev, top, planes, cores, rows, width)
    core = lax.axis_index("core")
    other = lax.dynamic_index_in_dim(grouped, 1 - core, 3, keepdims=False)
    keep = lax.dynamic_index_in_dim(grouped, core, 3, keepdims=False)
    arrived = lax.ppermute(other, "core", [(0, 1), (1, 0)])
    return keep + arrived


def scatter_z(summed):
    sec_dev, top, rows, width = summed.shape[0], summed.shape[1], summed.shape[3], summed.shape[4]
    total = lax.psum_scatter(summed, "z", scatter_dimension=2, tiled=True)
    return total.reshape(sec_dev, top, rows, width)


def solution(mesh):
    sec_size, mpo_size = mesh.devices.shape
    split = jax.sharding.Mesh(mesh.devices.reshape(sec_size, mpo_size // 2, 2), ("sec", "z", "core"))
    mpo = ("z", "core")
    return jax.shard_map(
        shards,
        mesh=split,
        in_specs=(
            P("sec", None, None, None),
            P(mpo, "sec", None, None),
            P(mpo, "sec", None, None),
            P(mpo, None),
            P(),
            P(),
            P(),
        ),
        out_specs=P("sec", None, mpo, None),
        check_vma=False,
    )
```
